512 devices in a mesh: chan: 16 (over y, core), tm: 32 (over z, x).
Axes of the slice: x: 4, y: 8, z: 8, core: 2. Of those that a mesh axis runs over, the one named last changes fastest.
Arguments:
- spike_sample: int32 [16, 131072], P('chan', 'tm'), may hold values from 0 to 245759, as said below
- spike_unit: int32 [16, 131072], P('chan', 'tm'), may hold values from 0 to 6143, as said below
- spike_amp: bfloat16 [16, 131072], P('chan', 'tm'), may hold values from 0.2 to 12, as said below
- pair_units: int32 [2, 16384], P(None, 'chan'), may hold values from 0 to 6143, as said below
Outputs:
- corr: float32 [101, 16384], P(None, ('chan', 'tm'))
The draws below stay inside these ranges and needn't reach their ends.
Inputs may be any that keep to these rules, and one draw needn't show every extreme that they name: `spike_sample`: the spike in column c of a row lies in time shard s = c // 4096: its sample index is at least s * 256 * 30 and below (s + 1) * 256 * 30. `spike_unit`: row g holds only spikes of units g * 384 to (g + 1) * 384 - 1. `spike_amp`: amplitudes are positive. `pair_units`: column c belongs to group g = c // 1024: its first unit is a unit of group g; its second is a unit of group g or, unless g is the last group, one of the first 64 units of group g + 1.
All inputs are finite; a program needn't handle non-finite values.
Results may differ from the reference program's by a relative error of at most 0.0031.
Values may be sent and summed in bfloat16 or wider, within the bound.
No kernel may reach another device: no remote copies, remote signals or barrier semaphores. Data moves between devices by JAX's collectives and lax.ppermute only.
A program may use at most 64 MiB of HBM per device.

```python
import math
import jax
import jax.numpy as jnp
from jax import lax

U_GRP = 384
BORDER = 64
BINS_DEV = 256
S_DEV = 4096
P_GRP = 1024
MAXLAG = 50
SPB = 30
UNITS = 6144
TIME = 8192
SPIKES = 131072
PAIRS = 16384
N_CHAN = 16
N_TM = 32


def unit_table(key):
    first_draw = jax.random.randint(jax.random.fold_in(key, 11), (N_CHAN, SPIKES), 0, U_GRP)
    second_draw = jax.random.randint(jax.random.fold_in(key, 12), (N_CHAN, SPIKES), 0, U_GRP)
    smaller = jnp.minimum(first_draw, second_draw)
    orders = jax.vmap(lambda k: jax.random.permutation(k, U_GRP))(jax.random.split(jax.random.fold_in(key, 13), N_CHAN))
    within = jnp.take_along_axis(orders, smaller, axis=1)
    column = jnp.arange(SPIKES)[None, :]
    within = jnp.where(column == 0, 0, jnp.where(column == SPIKES - 1, U_GRP - 1, within))
    return (within + jnp.arange(N_CHAN)[:, None] * U_GRP).astype(jnp.int32)


def draw_spike_unit(key, part):
    return unit_table(key)


def draw_spike_sample(key, part):
    span = BINS_DEV * SPB
    offsets = jax.random.randint(jax.random.fold_in(key, 31), (N_CHAN, SPIKES), 0, span)
    column = jnp.arange(SPIKES)[None, :]
    samples = column // S_DEV * span + offsets
    samples = jnp.where(column == 0, 0, jnp.where(column == SPIKES - 1, SPIKES // S_DEV * span - 1, samples))
    return samples.astype(jnp.int32)


def draw_spike_amp(key, part):
    units = unit_table(key)
    scales = jnp.exp(jax.random.uniform(jax.random.fold_in(key, 21), (UNITS,), jnp.float32, math.log(0.3), math.log(3.0)))
    base_amp = scales[units]
    column = jnp.arange(SPIKES)[None, :]
    shards = SPIKES // S_DEV
    drift = 1.0 + 2.0 * (column // S_DEV).astype(jnp.float32) / max(shards - 1, 1)
    jitter = jnp.exp(jnp.clip(0.25 * jax.random.normal(jax.random.fold_in(key, 22), (N_CHAN, SPIKES), jnp.float32), -0.26, 0.26))
    return (base_amp * drift * jitter).astype(jnp.bfloat16)


def draw_pair_units(key, part):
    column = jnp.arange(PAIRS)
    groups = column // P_GRP
    chans = PAIRS // P_GRP
    first_unit = jax.random.randint(jax.random.fold_in(key, 41), (PAIRS,), 0, U_GRP)
    other_unit = jax.random.randint(jax.random.fold_in(key, 42), (PAIRS,), 0, U_GRP)
    border_unit = U_GRP + jax.random.randint(jax.random.fold_in(key, 43), (PAIRS,), 0, BORDER)
    chooser = jax.random.randint(jax.random.fold_in(key, 44), (PAIRS,), 0, 4)
    second_unit = jnp.where((chooser == 0) & (groups < chans - 1), border_unit, jnp.where(chooser == 1, first_unit, other_unit))
    second_unit = jnp.where(column == PAIRS - 1, U_GRP - 1, second_unit)
    first_unit = jnp.where(column == 0, 0, first_unit)
    return jnp.stack([first_unit + groups * U_GRP, second_unit + groups * U_GRP]).astype(jnp.int32)


def setup_inputs(seed: int = 0) -> dict:
    arg_keys = jax.random.split(jax.random.key(seed), 5)
    spike_sample = draw_spike_sample(jax.random.fold_in(arg_keys[4], 71), 0)
    spike_unit = draw_spike_unit(jax.random.fold_in(arg_keys[4], 71), 0)
    spike_amp = draw_spike_amp(jax.random.fold_in(arg_keys[4], 71), 0)
    pair_units = draw_pair_units(jax.random.fold_in(arg_keys[4], 71), 0)
    return {"spike_sample": spike_sample, "spike_unit": spike_unit, "spike_amp": spike_amp, "pair_units": pair_units}


def lag_window(left_rows, right_rows):
    width = left_rows.shape[1]
    windows = jnp.stack([right_rows[:, k:k + width] for k in range(2 * MAXLAG + 1)], axis=1)
    return jnp.einsum("nt,nlt->nl", left_rows.astype(jnp.float32), windows.astype(jnp.float32))


def centred_group(group_index, spike_sample, spike_unit, spike_amp):
    samples = lax.dynamic_index_in_dim(spike_sample, group_index, 0, keepdims=False)
    units = lax.dynamic_index_in_dim(spike_unit, group_index, 0, keepdims=False)
    amplitudes = lax.dynamic_index_in_dim(spike_amp, group_index, 0, keepdims=False)
    within = (units - group_index * U_GRP).astype(jnp.int32)
    bin_index = (samples // SPB).astype(jnp.int32)
    trains = jnp.zeros((U_GRP, TIME), jnp.float32).at[within, bin_index].add(amplitudes.astype(jnp.float32))
    means = jnp.sum(trains, axis=1) / float(TIME)
    return (trains - means[:, None]).astype(jnp.bfloat16)


def reference(spike_sample, spike_unit, spike_amp, pair_units):
    def per_group(group_index):
        own_rows = centred_group(group_index, spike_sample, spike_unit, spike_amp)
        next_index = jnp.minimum(group_index + 1, N_CHAN - 1).astype(jnp.int32)
        next_rows = centred_group(next_index, spike_sample, spike_unit, spike_amp)
        border_rows = jnp.where(group_index < N_CHAN - 1, next_rows[:BORDER], jnp.zeros_like(next_rows[:BORDER]))
        extended = jnp.concatenate([own_rows, border_rows], axis=0)
        padded = jnp.pad(extended, ((0, 0), (MAXLAG, MAXLAG)))
        pair_block = lax.dynamic_slice(pair_units, (jnp.int32(0), (group_index * P_GRP).astype(jnp.int32)), (2, P_GRP))
        first_units = (pair_block[0] - group_index * U_GRP).astype(jnp.int32)
        second_units = (pair_block[1] - group_index * U_GRP).astype(jnp.int32)
        left_all = jnp.take(own_rows, first_units, axis=0)
        right_all = jnp.take(padded, second_units, axis=0)

        def step(running, shard_index):
            start_bin = (shard_index * BINS_DEV).astype(jnp.int32)
            left_rows = lax.dynamic_slice_in_dim(left_all, start_bin, BINS_DEV, 1)
            right_rows = lax.dynamic_slice_in_dim(right_all, start_bin, BINS_DEV + 2 * MAXLAG, 1)
            return running + lag_window(left_rows, right_rows), None

        running, unused = lax.scan(step, jnp.zeros((P_GRP, 2 * MAXLAG + 1), jnp.float32), jnp.arange(N_TM, dtype=jnp.int32))
        return running.T

    results = lax.map(per_group, jnp.arange(N_CHAN, dtype=jnp.int32))
    return jnp.transpose(results, (1, 0, 2)).reshape(2 * MAXLAG + 1, PAIRS)
```

```python
import jax
import jax.numpy as jnp
from jax import lax
from jax.experimental import pallas as pl
from jax.sharding import PartitionSpec as P

U_GRP = 384
BORDER = 64
BINS_DEV = 256
MAXLAG = 50
SPB = 30
NLAG = 2 * MAXLAG + 1
LANES = 128
KCHUNK = 16


def corr_kernel(l_ref, r_ref, o_ref):
    steps = l_ref.shape[0] // 8
    for first in range(0, NLAG, KCHUNK):
        lags = list(range(first, min(first + KCHUNK, NLAG)))

        def body(i, accs):
            t = pl.multiple_of(i * 8, 8)
            left = l_ref[pl.ds(t, 8), :]
            return tuple(a + left * r_ref[pl.ds(t + k, 8), :] for a, k in zip(accs, lags))

        accs = lax.fori_loop(
            0, steps, body, tuple(jnp.zeros((8, LANES), jnp.float32) for _ in lags)
        )
        for a, k in zip(accs, lags):
            o_ref[pl.ds(k, 1), :] = jnp.sum(a, axis=0, keepdims=True)


def lagged_products(left_t, right_t):
    pairs = left_t.shape[1]
    return pl.pallas_call(
        corr_kernel,
        grid=(pairs // LANES,),
        in_specs=[
            pl.BlockSpec((left_t.shape[0], LANES), lambda j: (0, j)),
            pl.BlockSpec((right_t.shape[0], LANES), lambda j: (0, j)),
        ],
        out_specs=pl.BlockSpec((NLAG, LANES), lambda j: (0, j)),
        out_shape=jax.ShapeDtypeStruct((NLAG, pairs), jnp.float32),
        cost_estimate=pl.CostEstimate(
            flops=2 * NLAG * pairs * left_t.shape[0],
            bytes_accessed=4 * pairs * (left_t.shape[0] + right_t.shape[0] + NLAG),
            transcendentals=0,
        ),
    )(left_t, right_t)


def summed_over(values, axis):
    peers = lax.axis_size(axis)
    spread = jnp.broadcast_to(values[None], (peers,) + values.shape)
    return jnp.sum(lax.all_to_all(spread, axis, 0, 0, tiled=False), axis=0)


def gather_columns(rows, index):
    onehot = (lax.broadcasted_iota(jnp.int32, (rows.shape[0], index.shape[0]), 0) == index[None, :])
    return lax.dot_general(
        rows, onehot.astype(rows.dtype), (((0,), (0,)), ((), ())),
        preferred_element_type=jnp.float32,
    )


def local(spike_sample, spike_unit, spike_amp, pair_units):
    group_index = lax.axis_index("chan")
    shard_index = lax.axis_index("tm")
    shard_count = lax.axis_size("tm")
    group_count = lax.axis_size("chan")

    bin_index = spike_sample[0] // SPB - shard_index * BINS_DEV
    within = spike_unit[0] - group_index * U_GRP
    unit_onehot = (within[None, :] == jnp.arange(U_GRP, dtype=jnp.int32)[:, None]).astype(
        jnp.bfloat16
    )
    weighted = jnp.where(
        bin_index[:, None] == jnp.arange(BINS_DEV, dtype=jnp.int32)[None, :],
        spike_amp[0][:, None],
        jnp.zeros((), jnp.bfloat16),
    )
    trains = jnp.dot(unit_onehot, weighted, preferred_element_type=jnp.float32)

    to_next = [(i, i + 1) for i in range(shard_count - 1)]
    to_prev = [(i + 1, i) for i in range(shard_count - 1)]
    left_raw = lax.ppermute(trains[:, BINS_DEV - MAXLAG :], "tm", to_next)
    right_raw = lax.ppermute(trains[:, :MAXLAG], "tm", to_prev)

    totals = summed_over(jnp.sum(trains, axis=1), "tm")
    means = totals / float(BINS_DEV * shard_count)

    def centre(x):
        return (x - means[:, None]).astype(jnp.bfloat16)

    zero = jnp.zeros((), jnp.bfloat16)
    left_halo = jnp.where(shard_index > 0, centre(left_raw), zero)
    right_halo = jnp.where(shard_index < shard_count - 1, centre(right_raw), zero)
    centred = centre(trains)
    padded_own = jnp.concatenate([left_halo, centred, right_halo], axis=1)
    border = lax.ppermute(
        padded_own[:BORDER], "chan", [(i + 1, i) for i in range(group_count - 1)]
    )
    padded = jnp.concatenate([padded_own, border], axis=0)

    first_units = pair_units[0] - group_index * U_GRP
    second_units = pair_units[1] - group_index * U_GRP
    left_t = gather_columns(centred, first_units)
    right_t = gather_columns(padded, second_units)
    partial = lagged_products(left_t, right_t)

    per_shard = partial.shape[1] // shard_count
    blocks = jnp.transpose(partial.reshape(NLAG, shard_count, per_shard), (1, 0, 2))
    return jnp.sum(lax.all_to_all(blocks, "tm", 0, 0, tiled=False), axis=0)


def solution(mesh):
    in_specs = (P("chan", "tm"), P("chan", "tm"), P("chan", "tm"), P(None, "chan"))
    out_specs = P(None, ("chan", "tm"))
    return jax.shard_map(local, mesh=mesh, in_specs=in_specs, out_specs=out_specs, check_vma=False)
```

```python
import jax
import jax.numpy as jnp
from jax import lax
from jax.experimental import pallas as pl
from jax.experimental.pallas import tpu as pltpu
from jax.sharding import PartitionSpec as P

U_GRP = 384
BORDER = 64
BINS_DEV = 256
MAXLAG = 50
SPB = 30
NLAG = 2 * MAXLAG + 1
LANES = 128
KCHUNK = 13


def corr_kernel(l_ref, r_ref, o_ref, shifted_ref):
    steps = l_ref.shape[0] // 8
    width = shifted_ref.shape[1]
    for r in range(8):
        shifted_ref[r] = r_ref[pl.ds(r, width), :]
    for first in range(0, NLAG, KCHUNK):
        lags = list(range(first, min(first + KCHUNK, NLAG)))

        def body(i, accs):
            t = pl.multiple_of(i * 8, 8)
            left = l_ref[pl.ds(t, 8), :]
            return tuple(
                a + left * shifted_ref[k % 8, pl.ds(t + 8 * (k // 8), 8), :]
                for a, k in zip(accs, lags)
            )

        accs = lax.fori_loop(
            0, steps, body, tuple(jnp.zeros((8, LANES), jnp.float32) for _ in lags),
            unroll=True,
        )
        for a, k in zip(accs, lags):
            o_ref[pl.ds(k, 1), :] = jnp.sum(a, axis=0, keepdims=True)


def lagged_products(left_t, right_t):
    pairs = left_t.shape[1]
    return pl.pallas_call(
        corr_kernel,
        grid=(pairs // LANES,),
        in_specs=[
            pl.BlockSpec((left_t.shape[0], LANES), lambda j: (0, j)),
            pl.BlockSpec((right_t.shape[0], LANES), lambda j: (0, j)),
        ],
        out_specs=pl.BlockSpec((NLAG, LANES), lambda j: (0, j)),
        out_shape=jax.ShapeDtypeStruct((NLAG, pairs), jnp.float32),
        scratch_shapes=[pltpu.VMEM((8, left_t.shape[0] + 96, LANES), jnp.float32)],
        cost_estimate=pl.CostEstimate(
            flops=2 * NLAG * pairs * left_t.shape[0],
            bytes_accessed=4 * pairs * (left_t.shape[0] + right_t.shape[0] + NLAG),
            transcendentals=0,
        ),
    )(left_t, right_t)


def summed_over(values, axis):
    peers = lax.axis_size(axis)
    spread = jnp.broadcast_to(values[None], (peers,) + values.shape)
    return jnp.sum(lax.all_to_all(spread, axis, 0, 0, tiled=False), axis=0)


def gather_columns(rows, index):
    onehot = (lax.broadcasted_iota(jnp.int32, (rows.shape[0], index.shape[0]), 0) == index[None, :])
    return lax.dot_general(
        rows, onehot.astype(rows.dtype), (((0,), (0,)), ((), ())),
        preferred_element_type=jnp.float32,
    )


def local(spike_sample, spike_unit, spike_amp, pair_units):
    group_index = lax.axis_index("chan")
    shard_index = lax.axis_index("tm")
    shard_count = lax.axis_size("tm")
    group_count = lax.axis_size("chan")

    bin_index = spike_sample[0] // SPB - shard_index * BINS_DEV
    within = spike_unit[0] - group_index * U_GRP
    unit_onehot = (within[None, :] == jnp.arange(U_GRP, dtype=jnp.int32)[:, None]).astype(
        jnp.bfloat16
    )
    weighted = jnp.where(
        bin_index[:, None] == jnp.arange(BINS_DEV, dtype=jnp.int32)[None, :],
        spike_amp[0][:, None],
        jnp.zeros((), jnp.bfloat16),
    )
    trains = jnp.dot(unit_onehot, weighted, preferred_element_type=jnp.float32)

    to_next = [(i, i + 1) for i in range(shard_count - 1)]
    to_prev = [(i + 1, i) for i in range(shard_count - 1)]
    left_raw = lax.ppermute(trains[:, BINS_DEV - MAXLAG :], "tm", to_next)
    right_raw = lax.ppermute(trains[:, :MAXLAG], "tm", to_prev)

    totals = summed_over(jnp.sum(trains, axis=1), "tm")
    means = totals / float(BINS_DEV * shard_count)

    def centre(x):
        return (x - means[:, None]).astype(jnp.bfloat16)

    zero = jnp.zeros((), jnp.bfloat16)
    left_halo = jnp.where(shard_index > 0, centre(left_raw), zero)
    right_halo = jnp.where(shard_index < shard_count - 1, centre(right_raw), zero)
    centred = centre(trains)
    tail_pad = jnp.zeros((U_GRP, 4), jnp.bfloat16)
    padded_own = jnp.concatenate([left_halo, centred, right_halo, tail_pad], axis=1)
    border = lax.ppermute(
        padded_own[:BORDER], "chan", [(i + 1, i) for i in range(group_count - 1)]
    )
    padded = jnp.concatenate([padded_own, border], axis=0)

    first_units = pair_units[0] - group_index * U_GRP
    second_units = pair_units[1] - group_index * U_GRP
    left_t = gather_columns(centred, first_units)
    right_t = gather_columns(padded, second_units)
    partial = lagged_products(left_t, right_t)

    per_shard = partial.shape[1] // shard_count
    blocks = jnp.transpose(partial.reshape(NLAG, shard_count, per_shard), (1, 0, 2))
    return jnp.sum(lax.all_to_all(blocks, "tm", 0, 0, tiled=False), axis=0)


def solution(mesh):
    in_specs = (P("chan", "tm"), P("chan", "tm"), P("chan", "tm"), P(None, "chan"))
    out_specs = P(None, ("chan", "tm"))
    return jax.shard_map(local, mesh=mesh, in_specs=in_specs, out_specs=out_specs, check_vma=False)
```

```python
import jax
import jax.numpy as jnp
from jax import lax
from jax.experimental import pallas as pl
from jax.experimental.pallas import tpu as pltpu
from jax.sharding import PartitionSpec as P

U_GRP = 384
BORDER = 64
BINS_DEV = 256
MAXLAG = 50
SPB = 30
NLAG = 2 * MAXLAG + 1
LANES = 128
KCHUNK = 13


def corr_kernel(l_ref, r_ref, o_ref, shifted_ref, lags_ref):
    steps = l_ref.shape[0] // 8
    width = shifted_ref.shape[1]
    for r in range(8):
        shifted_ref[r] = r_ref[pl.ds(r, width), :]
    for first in range(0, NLAG, KCHUNK):
        lags = list(range(first, min(first + KCHUNK, NLAG)))

        def body(i, accs):
            t = pl.multiple_of(i * 8, 8)
            left = l_ref[pl.ds(t, 8), :]
            return tuple(
                a + left * shifted_ref[k % 8, pl.ds(t + 8 * (k // 8), 8), :]
                for a, k in zip(accs, lags)
            )

        accs = lax.fori_loop(
            0, steps, body, tuple(jnp.zeros((8, LANES), jnp.float32) for _ in lags),
            unroll=True,
        )
        for a, k in zip(accs, lags):
            lags_ref[pl.ds(k, 1), :] = jnp.sum(a, axis=0, keepdims=True)
    lags_ref[pl.ds(NLAG, LANES - NLAG), :] = jnp.zeros((LANES - NLAG, LANES), jnp.float32)
    o_ref[...] = lags_ref[...].T


def lagged_products(left_t, right_t):
    pairs = left_t.shape[1]
    return pl.pallas_call(
        corr_kernel,
        grid=(pairs // LANES,),
        in_specs=[
            pl.BlockSpec((left_t.shape[0], LANES), lambda j: (0, j)),
            pl.BlockSpec((right_t.shape[0], LANES), lambda j: (0, j)),
        ],
        out_specs=pl.BlockSpec((LANES, LANES), lambda j: (j, 0)),
        out_shape=jax.ShapeDtypeStruct((pairs, LANES), jnp.float32),
        scratch_shapes=[
            pltpu.VMEM((8, left_t.shape[0] + 96, LANES), jnp.float32),
            pltpu.VMEM((LANES, LANES), jnp.float32),
        ],
        cost_estimate=pl.CostEstimate(
            flops=2 * NLAG * pairs * left_t.shape[0],
            bytes_accessed=4 * pairs * (left_t.shape[0] + right_t.shape[0] + LANES),
            transcendentals=0,
        ),
    )(left_t, right_t)


def summed_over(values, axis):
    peers = lax.axis_size(axis)
    spread = jnp.broadcast_to(values[None], (peers,) + values.shape)
    return jnp.sum(lax.all_to_all(spread, axis, 0, 0, tiled=False), axis=0)


def gather_columns(rows, index):
    onehot = (lax.broadcasted_iota(jnp.int32, (rows.shape[0], index.shape[0]), 0) == index[None, :])
    return lax.dot_general(
        rows, onehot.astype(rows.dtype), (((0,), (0,)), ((), ())),
        preferred_element_type=jnp.float32,
    )


def local(spike_sample, spike_unit, spike_amp, pair_units):
    group_index = lax.axis_index("chan")
    shard_index = lax.axis_index("tm")
    shard_count = lax.axis_size("tm")
    group_count = lax.axis_size("chan")

    bin_index = lax.div(spike_sample, SPB) - shard_index * BINS_DEV
    within = spike_unit - group_index * U_GRP
    unit_onehot = (within == lax.broadcasted_iota(jnp.int32, (U_GRP, 1), 0)).astype(jnp.bfloat16)
    weighted = jnp.where(
        bin_index == lax.broadcasted_iota(jnp.int32, (BINS_DEV, 1), 0),
        spike_amp,
        jnp.zeros((), jnp.bfloat16),
    )
    trains = lax.dot_general(
        unit_onehot, weighted, (((1,), (1,)), ((), ())), preferred_element_type=jnp.float32
    )

    to_next = [(i, i + 1) for i in range(shard_count - 1)]
    to_prev = [(i + 1, i) for i in range(shard_count - 1)]
    left_raw = lax.ppermute(trains[:, BINS_DEV - MAXLAG :], "tm", to_next)
    right_raw = lax.ppermute(trains[:, :MAXLAG], "tm", to_prev)

    totals = summed_over(jnp.sum(trains, axis=1), "tm")
    means = totals / float(BINS_DEV * shard_count)

    def centre(x):
        return (x - means[:, None]).astype(jnp.bfloat16)

    zero = jnp.zeros((), jnp.bfloat16)
    left_halo = jnp.where(shard_index > 0, centre(left_raw), zero)
    right_halo = jnp.where(shard_index < shard_count - 1, centre(right_raw), zero)
    centred = centre(trains)
    tail_pad = jnp.zeros((U_GRP, 4), jnp.bfloat16)
    padded_own = jnp.concatenate([left_halo, centred, right_halo, tail_pad], axis=1)
    border = lax.ppermute(
        padded_own[:BORDER], "chan", [(i + 1, i) for i in range(group_count - 1)]
    )
    padded = jnp.concatenate([padded_own, border], axis=0)

    first_units = pair_units[0] - group_index * U_GRP
    second_units = pair_units[1] - group_index * U_GRP
    left_t = gather_columns(centred, first_units)
    right_t = gather_columns(padded, second_units)
    partial = lagged_products(left_t, right_t)

    per_shard = partial.shape[0] // shard_count
    blocks = partial.reshape(shard_count, per_shard, LANES)
    summed = jnp.sum(lax.all_to_all(blocks, "tm", 0, 0, tiled=False), axis=0)
    return summed[:, :NLAG].T


def solution(mesh):
    in_specs = (P("chan", "tm"), P("chan", "tm"), P("chan", "tm"), P(None, "chan"))
    out_specs = P(None, ("chan", "tm"))
    return jax.shard_map(local, mesh=mesh, in_specs=in_specs, out_specs=out_specs, check_vma=False)
```

```python
import jax
import jax.numpy as jnp
from jax import lax
from jax.experimental import pallas as pl
from jax.experimental.pallas import tpu as pltpu
from jax.sharding import PartitionSpec as P

U_GRP = 384
BORDER = 64
BINS_DEV = 256
MAXLAG = 50
SPB = 30
NLAG = 2 * MAXLAG + 1
LANES = 128
KCHUNK = 13


def corr_kernel(l_ref, r_ref, o_ref, shifted_ref, lags_ref):
    steps = l_ref.shape[0] // 8
    width = shifted_ref.shape[1]
    for r in range(8):
        shifted_ref[r] = r_ref[pl.ds(r, width), :]
    for first in range(0, NLAG, KCHUNK):
        lags = list(range(first, min(first + KCHUNK, NLAG)))

        def body(i, accs):
            t = pl.multiple_of(i * 8, 8)
            left = l_ref[pl.ds(t, 8), :]
            return tuple(
                a + left * shifted_ref[k % 8, pl.ds(t + 8 * (k // 8), 8), :]
                for a, k in zip(accs, lags)
            )

        accs = lax.fori_loop(
            0, steps, body, tuple(jnp.zeros((8, LANES), jnp.float32) for _ in lags),
            unroll=True,
        )
        for a, k in zip(accs, lags):
            lags_ref[pl.ds(k, 1), :] = jnp.sum(a, axis=0, keepdims=True)
    lags_ref[pl.ds(NLAG, LANES - NLAG), :] = jnp.zeros((LANES - NLAG, LANES), jnp.float32)
    o_ref[...] = lags_ref[...].T


def lagged_products(left_t, right_t):
    pairs = left_t.shape[1]
    return pl.pallas_call(
        corr_kernel,
        grid=(pairs // LANES,),
        in_specs=[
            pl.BlockSpec((left_t.shape[0], LANES), lambda j: (0, j)),
            pl.BlockSpec((right_t.shape[0], LANES), lambda j: (0, j)),
        ],
        out_specs=pl.BlockSpec((LANES, LANES), lambda j: (j, 0)),
        out_shape=jax.ShapeDtypeStruct((pairs, LANES), jnp.float32),
        scratch_shapes=[
            pltpu.VMEM((8, left_t.shape[0] + 96, LANES), jnp.float32),
            pltpu.VMEM((LANES, LANES), jnp.float32),
        ],
        cost_estimate=pl.CostEstimate(
            flops=2 * NLAG * pairs * left_t.shape[0],
            bytes_accessed=4 * pairs * (left_t.shape[0] + right_t.shape[0] + LANES),
            transcendentals=0,
        ),
    )(left_t, right_t)


def summed_over(values, axis):
    peers = lax.axis_size(axis)
    spread = jnp.broadcast_to(values[None], (peers,) + values.shape)
    return jnp.sum(lax.all_to_all(spread, axis, 0, 0, tiled=False), axis=0)


def gather_columns(rows, index):
    onehot = (lax.broadcasted_iota(jnp.int32, (rows.shape[0], index.shape[0]), 0) == index[None, :])
    return lax.dot_general(
        rows, onehot.astype(rows.dtype), (((0,), (0,)), ((), ())),
        preferred_element_type=jnp.float32,
    )


def local(spike_sample, spike_unit, spike_amp, pair_units):
    group_index = lax.axis_index("chan")
    shard_index = lax.axis_index("tm")
    shard_count = lax.axis_size("tm")
    group_count = lax.axis_size("chan")

    bin_index = lax.div(spike_sample, SPB) - shard_index * BINS_DEV
    within = spike_unit - group_index * U_GRP
    unit_onehot = (within == lax.broadcasted_iota(jnp.int32, (U_GRP, 1), 0)).astype(jnp.bfloat16)
    weighted = jnp.where(
        bin_index == lax.broadcasted_iota(jnp.int32, (BINS_DEV, 1), 0),
        spike_amp,
        jnp.zeros((), jnp.bfloat16),
    )
    trains = lax.dot_general(
        unit_onehot, weighted, (((1,), (1,)), ((), ())), preferred_element_type=jnp.float32
    )

    to_next = [(i, i + 1) for i in range(shard_count - 1)]
    to_prev = [(i + 1, i) for i in range(shard_count - 1)]
    left_raw = lax.ppermute(trains[:, BINS_DEV - MAXLAG :], "tm", to_next)
    right_raw = lax.ppermute(trains[:, :MAXLAG], "tm", to_prev)

    totals = summed_over(jnp.sum(trains, axis=1), "tm")
    means = totals / float(BINS_DEV * shard_count)

    def centre(x):
        return (x - means[:, None]).astype(jnp.bfloat16)

    zero = jnp.zeros((), jnp.bfloat16)
    left_halo = jnp.where(shard_index > 0, centre(left_raw), zero)
    right_halo = jnp.where(shard_index < shard_count - 1, centre(right_raw), zero)
    centred = centre(trains)
    tail_pad = jnp.zeros((U_GRP, 4), jnp.bfloat16)
    padded_own = jnp.concatenate([left_halo, centred, right_halo, tail_pad], axis=1)
    border = lax.ppermute(
        padded_own[:BORDER], "chan", [(i + 1, i) for i in range(group_count - 1)]
    )
    padded = jnp.concatenate([padded_own, border], axis=0)

    per_shard = pair_units.shape[1] // shard_count
    halves = 2

    def in_halves(index):
        return jnp.transpose(
            index.reshape(shard_count, halves, per_shard // halves), (1, 0, 2)
        ).reshape(halves, -1)

    first_units = in_halves(pair_units[0] - group_index * U_GRP)
    second_units = in_halves(pair_units[1] - group_index * U_GRP)
    summed = []
    for h in range(halves):
        left_t = gather_columns(centred, first_units[h])
        right_t = gather_columns(padded, second_units[h])
        partial = lagged_products(left_t, right_t)
        blocks = partial.reshape(shard_count, per_shard // halves, LANES)
        summed.append(jnp.sum(lax.all_to_all(blocks, "tm", 0, 0, tiled=False), axis=0))
    return jnp.concatenate(summed, axis=0)[:, :NLAG].T


def solution(mesh):
    in_specs = (P("chan", "tm"), P("chan", "tm"), P("chan", "tm"), P(None, "chan"))
    out_specs = P(None, ("chan", "tm"))
    return jax.shard_map(local, mesh=mesh, in_specs=in_specs, out_specs=out_specs, check_vma=False)
```

```python
import jax
import jax.numpy as jnp
from jax import lax
from jax.experimental import pallas as pl
from jax.experimental.pallas import tpu as pltpu
from jax.sharding import PartitionSpec as P

U_GRP = 384
BORDER = 64
BINS_DEV = 256
MAXLAG = 50
SPB = 30
NLAG = 2 * MAXLAG + 1
LANES = 128
KCHUNK = 13
WINDOW_PAD = 6


def corr_kernel(l_ref, r_ref, o_ref, left_ref, right_ref, lags_ref):
    steps = (l_ref.shape[0] - MAXLAG) // 8
    width = left_ref.shape[1]
    for r in range(8):
        left_ref[r] = l_ref[pl.ds(r, width), :]
        right_ref[r] = r_ref[pl.ds(r, width), :]

    def lag_rows(fixed_ref, moving_ref, lags, shift_of):
        def body(i, accs):
            t = pl.multiple_of(i * 8, 8)
            fixed = fixed_ref[MAXLAG % 8, pl.ds(t + 8 * (MAXLAG // 8), 8), :]
            return tuple(
                a + fixed * moving_ref[shift_of(k) % 8, pl.ds(t + 8 * (shift_of(k) // 8), 8), :]
                for a, k in zip(accs, lags)
            )

        accs = lax.fori_loop(
            0, steps, body, tuple(jnp.zeros((8, LANES), jnp.float32) for _ in lags),
            unroll=True,
        )
        for a, k in zip(accs, lags):
            lags_ref[pl.ds(k, 1), :] = jnp.sum(a, axis=0, keepdims=True)

    for first in range(0, MAXLAG, KCHUNK):
        lag_rows(left_ref, right_ref, list(range(first, min(first + KCHUNK, MAXLAG))), lambda k: k)
    for first in range(MAXLAG, NLAG, KCHUNK):
        lag_rows(
            right_ref, left_ref, list(range(first, min(first + KCHUNK, NLAG))),
            lambda k: 2 * MAXLAG - k,
        )
    lags_ref[pl.ds(NLAG, LANES - NLAG), :] = jnp.zeros((LANES - NLAG, LANES), jnp.float32)
    o_ref[...] = lags_ref[...].T


def lagged_products(left_t, right_t):
    pairs = left_t.shape[1]
    bins = left_t.shape[0] - MAXLAG - WINDOW_PAD
    return pl.pallas_call(
        corr_kernel,
        grid=(pairs // LANES,),
        in_specs=[
            pl.BlockSpec((left_t.shape[0], LANES), lambda j: (0, j)),
            pl.BlockSpec((right_t.shape[0], LANES), lambda j: (0, j)),
        ],
        out_specs=pl.BlockSpec((LANES, LANES), lambda j: (j, 0)),
        out_shape=jax.ShapeDtypeStruct((pairs, LANES), jnp.float32),
        scratch_shapes=[
            pltpu.VMEM((8, left_t.shape[0] - 8, LANES), jnp.float32),
            pltpu.VMEM((8, left_t.shape[0] - 8, LANES), jnp.float32),
            pltpu.VMEM((LANES, LANES), jnp.float32),
        ],
        cost_estimate=pl.CostEstimate(
            flops=2 * NLAG * pairs * bins,
            bytes_accessed=4 * pairs * (left_t.shape[0] + right_t.shape[0] + LANES),
            transcendentals=0,
        ),
    )(left_t, right_t)


def summed_over(values, axis):
    peers = lax.axis_size(axis)
    spread = jnp.broadcast_to(values[None], (peers,) + values.shape)
    return jnp.sum(lax.all_to_all(spread, axis, 0, 0, tiled=False), axis=0)


def gather_columns(rows, index):
    onehot = (lax.broadcasted_iota(jnp.int32, (rows.shape[0], index.shape[0]), 0) == index[None, :])
    return lax.dot_general(
        rows, onehot.astype(rows.dtype), (((0,), (0,)), ((), ())),
        preferred_element_type=jnp.float32,
    )


def local(spike_sample, spike_unit, spike_amp, pair_units):
    group_index = lax.axis_index("chan")
    shard_index = lax.axis_index("tm")
    shard_count = lax.axis_size("tm")
    group_count = lax.axis_size("chan")

    bin_index = lax.div(spike_sample, SPB) - shard_index * BINS_DEV
    within = spike_unit - group_index * U_GRP
    unit_onehot = (within == lax.broadcasted_iota(jnp.int32, (U_GRP, 1), 0)).astype(jnp.bfloat16)
    weighted = jnp.where(
        bin_index == lax.broadcasted_iota(jnp.int32, (BINS_DEV, 1), 0),
        spike_amp,
        jnp.zeros((), jnp.bfloat16),
    )
    trains = lax.dot_general(
        unit_onehot, weighted, (((1,), (1,)), ((), ())), preferred_element_type=jnp.float32
    )

    to_next = [(i, i + 1) for i in range(shard_count - 1)]
    left_raw = lax.ppermute(trains[:, BINS_DEV - MAXLAG :], "tm", to_next)

    totals = summed_over(jnp.sum(trains, axis=1), "tm")
    means = totals / float(BINS_DEV * shard_count)

    def centre(x):
        return (x - means[:, None]).astype(jnp.bfloat16)

    left_halo = jnp.where(shard_index > 0, centre(left_raw), jnp.zeros((), jnp.bfloat16))
    window_own = jnp.concatenate(
        [left_halo, centre(trains), jnp.zeros((U_GRP, WINDOW_PAD), jnp.bfloat16)], axis=1
    )
    border = lax.ppermute(
        window_own[:BORDER], "chan", [(i + 1, i) for i in range(group_count - 1)]
    )
    window = jnp.concatenate([window_own, border], axis=0)

    first_units = pair_units[0] - group_index * U_GRP
    second_units = pair_units[1] - group_index * U_GRP
    left_t = gather_columns(window_own, first_units)
    right_t = gather_columns(window, second_units)
    partial = lagged_products(left_t, right_t)

    per_shard = partial.shape[0] // shard_count
    blocks = partial.reshape(shard_count, per_shard, LANES)
    summed = jnp.sum(lax.all_to_all(blocks, "tm", 0, 0, tiled=False), axis=0)
    return summed[:, :NLAG].T


def solution(mesh):
    in_specs = (P("chan", "tm"), P("chan", "tm"), P("chan", "tm"), P(None, "chan"))
    out_specs = P(None, ("chan", "tm"))
    return jax.shard_map(local, mesh=mesh, in_specs=in_specs, out_specs=out_specs, check_vma=False)
```

```python
import jax
import jax.numpy as jnp
from jax import lax
from jax.experimental import pallas as pl
from jax.experimental.pallas import tpu as pltpu
from jax.sharding import PartitionSpec as P

U_GRP = 384
BORDER = 64
BINS_DEV = 256
MAXLAG = 50
SPB = 30
NLAG = 2 * MAXLAG + 1
LANES = 128
KCHUNK = 13
WINDOW_PAD = 6


def corr_kernel(l_ref, r_ref, o_ref, left_ref, right_ref, lags_ref):
    steps = (l_ref.shape[0] - MAXLAG) // 8
    width = left_ref.shape[1]
    for r in range(8):
        left_ref[r] = l_ref[pl.ds(r, width), :]
        right_ref[r] = r_ref[pl.ds(r, width), :]

    def lag_rows(fixed_ref, moving_ref, lags, shift_of):
        def body(i, accs):
            t = pl.multiple_of(i * 8, 8)
            fixed = fixed_ref[MAXLAG % 8, pl.ds(t + 8 * (MAXLAG // 8), 8), :]
            return tuple(
                a + fixed * moving_ref[shift_of(k) % 8, pl.ds(t + 8 * (shift_of(k) // 8), 8), :]
                for a, k in zip(accs, lags)
            )

        accs = lax.fori_loop(
            0, steps, body, tuple(jnp.zeros((8, LANES), jnp.float32) for _ in lags),
            unroll=True,
        )
        for a, k in zip(accs, lags):
            lags_ref[pl.ds(k, 1), :] = jnp.sum(a, axis=0, keepdims=True)

    for first in range(0, MAXLAG, KCHUNK):
        lag_rows(left_ref, right_ref, list(range(first, min(first + KCHUNK, MAXLAG))), lambda k: k)
    for first in range(MAXLAG, NLAG, KCHUNK):
        lag_rows(
            right_ref, left_ref, list(range(first, min(first + KCHUNK, NLAG))),
            lambda k: 2 * MAXLAG - k,
        )
    lags_ref[pl.ds(NLAG, LANES - NLAG), :] = jnp.zeros((LANES - NLAG, LANES), jnp.float32)
    o_ref[...] = lags_ref[...].T


def lagged_products(left_t, right_t):
    pairs = left_t.shape[1]
    bins = left_t.shape[0] - MAXLAG - WINDOW_PAD
    return pl.pallas_call(
        corr_kernel,
        grid=(pairs // LANES,),
        in_specs=[
            pl.BlockSpec((left_t.shape[0], LANES), lambda j: (0, j)),
            pl.BlockSpec((right_t.shape[0], LANES), lambda j: (0, j)),
        ],
        out_specs=pl.BlockSpec((LANES, LANES), lambda j: (j, 0)),
        out_shape=jax.ShapeDtypeStruct((pairs, LANES), jnp.float32),
        scratch_shapes=[
            pltpu.VMEM((8, left_t.shape[0] - 8, LANES), jnp.float32),
            pltpu.VMEM((8, left_t.shape[0] - 8, LANES), jnp.float32),
            pltpu.VMEM((LANES, LANES), jnp.float32),
        ],
        cost_estimate=pl.CostEstimate(
            flops=2 * NLAG * pairs * bins,
            bytes_accessed=4 * pairs * (left_t.shape[0] + right_t.shape[0] + LANES),
            transcendentals=0,
        ),
    )(left_t, right_t)


def trains_kernel(offsets_ref, sample_ref, unit_ref, amp_ref, trains_ref, spread_ref):
    spikes = sample_ref.shape[1]
    bins = lax.div(sample_ref[...], SPB) - offsets_ref[1]
    within = unit_ref[...] - offsets_ref[0]
    amp = amp_ref[...]
    zero = jnp.zeros((), jnp.bfloat16)
    one = jnp.ones((), jnp.bfloat16)
    unit_onehot = jnp.where(within == lax.broadcasted_iota(jnp.int32, (U_GRP, spikes), 0), one, zero)
    weighted = jnp.where(bins == lax.broadcasted_iota(jnp.int32, (BINS_DEV, spikes), 0), amp, zero)
    trains_ref[...] = lax.dot_general(unit_onehot, weighted, (((1,), (1,)), ((), ())), preferred_element_type=jnp.float32)
    sums = lax.dot_general(jnp.broadcast_to(amp, (8, spikes)), unit_onehot, (((1,), (1,)), ((), ())), preferred_element_type=jnp.float32)
    spread_ref[...] = jnp.broadcast_to(sums[0:1], spread_ref.shape)

def trains_and_sums(offsets, sample, unit, amp, peers):
    spikes = sample.shape[1]
    return pl.pallas_call(
        trains_kernel,
        in_specs=[pl.BlockSpec(memory_space=pltpu.SMEM)]
        + [pl.BlockSpec(memory_space=pltpu.VMEM)] * 3,
        out_specs=[pl.BlockSpec(memory_space=pltpu.VMEM)] * 2,
        out_shape=[
            jax.ShapeDtypeStruct((U_GRP, BINS_DEV), jnp.float32),
            jax.ShapeDtypeStruct((peers, U_GRP), jnp.float32),
        ],
    )(offsets, sample, unit, amp)

def gather_columns(rows, index):
    onehot = (lax.broadcasted_iota(jnp.int32, (rows.shape[0], index.shape[0]), 0) == index[None, :])
    return lax.dot_general(
        rows, onehot.astype(rows.dtype), (((0,), (0,)), ((), ())),
        preferred_element_type=jnp.float32,
    )


def local(spike_sample, spike_unit, spike_amp, pair_units):
    group_index = lax.axis_index("chan")
    shard_index = lax.axis_index("tm")
    shard_count = lax.axis_size("tm")
    group_count = lax.axis_size("chan")

    offsets = jnp.stack([group_index * U_GRP, shard_index * BINS_DEV]).astype(jnp.int32)
    trains, spread = trains_and_sums(offsets, spike_sample, spike_unit, spike_amp, shard_count)

    to_next = [(i, i + 1) for i in range(shard_count - 1)]
    left_raw = lax.ppermute(trains[:, BINS_DEV - MAXLAG :], "tm", to_next)

    totals = jnp.sum(lax.all_to_all(spread[:, None, :], "tm", 0, 0, tiled=False), axis=(0, 1))
    means = totals / float(BINS_DEV * shard_count)

    def centre(x):
        return (x - means[:, None]).astype(jnp.bfloat16)

    left_halo = jnp.where(shard_index > 0, centre(left_raw), jnp.zeros((), jnp.bfloat16))
    window_own = jnp.concatenate(
        [left_halo, centre(trains), jnp.zeros((U_GRP, WINDOW_PAD), jnp.bfloat16)], axis=1
    )
    border = lax.ppermute(
        window_own[:BORDER], "chan", [(i + 1, i) for i in range(group_count - 1)]
    )
    window = jnp.concatenate([window_own, border], axis=0)

    first_units = pair_units[0] - group_index * U_GRP
    second_units = pair_units[1] - group_index * U_GRP
    left_t = gather_columns(window_own, first_units)
    right_t = gather_columns(window, second_units)
    partial = lagged_products(left_t, right_t)

    per_shard = partial.shape[0] // shard_count
    blocks = partial.reshape(shard_count, per_shard, LANES)
    summed = jnp.sum(lax.all_to_all(blocks, "tm", 0, 0, tiled=False), axis=0)
    return summed[:, :NLAG].T


def solution(mesh):
    in_specs = (P("chan", "tm"), P("chan", "tm"), P("chan", "tm"), P(None, "chan"))
    out_specs = P(None, ("chan", "tm"))
    return jax.shard_map(local, mesh=mesh, in_specs=in_specs, out_specs=out_specs, check_vma=False)
```

```python
import jax
import jax.numpy as jnp
from jax import lax
from jax.experimental import pallas as pl
from jax.experimental.pallas import tpu as pltpu
from jax.sharding import PartitionSpec as P

U_GRP = 384
BORDER = 64
BINS_DEV = 256
MAXLAG = 50
SPB = 30
NLAG = 2 * MAXLAG + 1
LANES = 128
KCHUNK = 13
WINDOW_PAD = 6


def corr_kernel(l_ref, r_ref, o_ref, left_ref, right_ref, lags_ref):
    steps = (l_ref.shape[0] - MAXLAG) // 8
    width = left_ref.shape[1]
    for r in range(8):
        left_ref[r] = l_ref[pl.ds(r, width), :]
        right_ref[r] = r_ref[pl.ds(r, width), :]

    def lag_rows(fixed_ref, moving_ref, lags, shift_of):
        def body(i, accs):
            t = pl.multiple_of(i * 8, 8)
            fixed = fixed_ref[MAXLAG % 8, pl.ds(t + 8 * (MAXLAG // 8), 8), :]
            return tuple(
                a + fixed * moving_ref[shift_of(k) % 8, pl.ds(t + 8 * (shift_of(k) // 8), 8), :]
                for a, k in zip(accs, lags)
            )

        accs = lax.fori_loop(
            0, steps, body, tuple(jnp.zeros((8, LANES), jnp.float32) for _ in lags),
            unroll=True,
        )
        for a, k in zip(accs, lags):
            lags_ref[pl.ds(k, 1), :] = jnp.sum(a, axis=0, keepdims=True)

    for first in range(0, MAXLAG, KCHUNK):
        lag_rows(left_ref, right_ref, list(range(first, min(first + KCHUNK, MAXLAG))), lambda k: k)
    for first in range(MAXLAG, NLAG, KCHUNK):
        lag_rows(
            right_ref, left_ref, list(range(first, min(first + KCHUNK, NLAG))),
            lambda k: 2 * MAXLAG - k,
        )
    lags_ref[pl.ds(NLAG, LANES - NLAG), :] = jnp.zeros((LANES - NLAG, LANES), jnp.float32)
    o_ref[...] = lags_ref[...].T


def lagged_products(left_t, right_t):
    pairs = left_t.shape[1]
    bins = left_t.shape[0] - MAXLAG - WINDOW_PAD
    return pl.pallas_call(
        corr_kernel,
        grid=(pairs // LANES,),
        in_specs=[
            pl.BlockSpec((left_t.shape[0], LANES), lambda j: (0, j)),
            pl.BlockSpec((right_t.shape[0], LANES), lambda j: (0, j)),
        ],
        out_specs=pl.BlockSpec((LANES, LANES), lambda j: (j, 0)),
        out_shape=jax.ShapeDtypeStruct((pairs, LANES), jnp.float32),
        scratch_shapes=[
            pltpu.VMEM((8, left_t.shape[0] - 8, LANES), jnp.float32),
            pltpu.VMEM((8, left_t.shape[0] - 8, LANES), jnp.float32),
            pltpu.VMEM((LANES, LANES), jnp.float32),
        ],
        cost_estimate=pl.CostEstimate(
            flops=2 * NLAG * pairs * bins,
            bytes_accessed=4 * pairs * (left_t.shape[0] + right_t.shape[0] + LANES),
            transcendentals=0,
        ),
    )(left_t, right_t)


def summed_over(values, axis):
    peers = lax.axis_size(axis)
    spread = jnp.broadcast_to(values[None], (peers,) + values.shape)
    return jnp.sum(lax.all_to_all(spread, axis, 0, 0, tiled=False), axis=0)


def gather_columns(rows, index):
    onehot = (lax.broadcasted_iota(jnp.int32, (rows.shape[0], index.shape[0]), 0) == index[None, :])
    return lax.dot_general(
        rows, onehot.astype(rows.dtype), (((0,), (0,)), ((), ())),
        preferred_element_type=jnp.float32,
    )


def local(spike_sample, spike_unit, spike_amp, pair_units):
    group_index = lax.axis_index("chan")
    shard_index = lax.axis_index("tm")
    shard_count = lax.axis_size("tm")
    group_count = lax.axis_size("chan")

    bin_index = lax.div(spike_sample, SPB) - shard_index * BINS_DEV
    within = spike_unit - group_index * U_GRP
    unit_onehot = (within == lax.broadcasted_iota(jnp.int32, (U_GRP, 1), 0)).astype(jnp.bfloat16)
    weighted = jnp.where(
        bin_index == lax.broadcasted_iota(jnp.int32, (BINS_DEV, 1), 0),
        spike_amp,
        jnp.zeros((), jnp.bfloat16),
    )
    trains = lax.optimization_barrier(
        lax.dot_general(
            unit_onehot, weighted, (((1,), (1,)), ((), ())), preferred_element_type=jnp.float32
        )
    )

    unit_sums = lax.dot_general(
        unit_onehot, spike_amp, (((1,), (1,)), ((), ())), preferred_element_type=jnp.float32
    )[:, 0]

    to_next = [(i, i + 1) for i in range(shard_count - 1)]
    left_raw = lax.ppermute(trains[:, BINS_DEV - MAXLAG :], "tm", to_next)

    totals = summed_over(unit_sums, "tm")
    means = totals / float(BINS_DEV * shard_count)

    def centre(x):
        return (x - means[:, None]).astype(jnp.bfloat16)

    left_halo = jnp.where(shard_index > 0, centre(left_raw), jnp.zeros((), jnp.bfloat16))
    window_own = jnp.concatenate(
        [left_halo, centre(trains), jnp.zeros((U_GRP, WINDOW_PAD), jnp.bfloat16)], axis=1
    )
    border = lax.ppermute(
        window_own[:BORDER], "chan", [(i + 1, i) for i in range(group_count - 1)]
    )
    window = jnp.concatenate([window_own, border], axis=0)

    first_units = pair_units[0] - group_index * U_GRP
    second_units = pair_units[1] - group_index * U_GRP
    left_t = gather_columns(window_own, first_units)
    right_t = gather_columns(window, second_units)
    partial = lagged_products(left_t, right_t)

    per_shard = partial.shape[0] // shard_count
    blocks = partial.reshape(shard_count, per_shard, LANES)
    summed = jnp.sum(lax.all_to_all(blocks, "tm", 0, 0, tiled=False), axis=0)
    return summed[:, :NLAG].T


def solution(mesh):
    in_specs = (P("chan", "tm"), P("chan", "tm"), P("chan", "tm"), P(None, "chan"))
    out_specs = P(None, ("chan", "tm"))
    return jax.shard_map(local, mesh=mesh, in_specs=in_specs, out_specs=out_specs, check_vma=False)
```

```python
import jax
import jax.numpy as jnp
from jax import lax
from jax.experimental import pallas as pl
from jax.experimental.pallas import tpu as pltpu
from jax.sharding import PartitionSpec as P

U_GRP = 384
BORDER = 64
BINS_DEV = 256
MAXLAG = 50
SPB = 30
NLAG = 2 * MAXLAG + 1
LANES = 128
KCHUNK = 13
WINDOW_PAD = 6


def corr_kernel(
    own_ref, all_ref, first_ref, second_ref, o_ref, l_ref, r_ref, left_ref, right_ref, lags_ref
):
    for units_ref, index_ref, out_ref in ((own_ref, first_ref, l_ref), (all_ref, second_ref, r_ref)):
        onehot = lax.broadcasted_iota(jnp.int32, (units_ref.shape[1], LANES), 0) == index_ref[...]
        out_ref[...] = jnp.dot(
            units_ref[...], onehot.astype(units_ref.dtype), preferred_element_type=jnp.float32
        )
    steps = (l_ref.shape[0] - MAXLAG) // 8
    width = left_ref.shape[1]
    for r in range(8):
        left_ref[r] = l_ref[pl.ds(r, width), :]
        right_ref[r] = r_ref[pl.ds(r, width), :]

    def lag_rows(fixed_ref, moving_ref, lags, shift_of):
        def body(i, accs):
            t = pl.multiple_of(i * 8, 8)
            fixed = fixed_ref[MAXLAG % 8, pl.ds(t + 8 * (MAXLAG // 8), 8), :]
            return tuple(
                a + fixed * moving_ref[shift_of(k) % 8, pl.ds(t + 8 * (shift_of(k) // 8), 8), :]
                for a, k in zip(accs, lags)
            )

        accs = lax.fori_loop(
            0, steps, body, tuple(jnp.zeros((8, LANES), jnp.float32) for _ in lags),
            unroll=True,
        )
        for a, k in zip(accs, lags):
            lags_ref[pl.ds(k, 1), :] = jnp.sum(a, axis=0, keepdims=True)

    for first in range(0, MAXLAG, KCHUNK):
        lag_rows(left_ref, right_ref, list(range(first, min(first + KCHUNK, MAXLAG))), lambda k: k)
    for first in range(MAXLAG, NLAG, KCHUNK):
        lag_rows(
            right_ref, left_ref, list(range(first, min(first + KCHUNK, NLAG))),
            lambda k: 2 * MAXLAG - k,
        )
    lags_ref[pl.ds(NLAG, LANES - NLAG), :] = jnp.zeros((LANES - NLAG, LANES), jnp.float32)
    o_ref[...] = lags_ref[...].T


def lagged_products(own_t, all_t, first_units, second_units):
    pairs = first_units.shape[1]
    window = own_t.shape[0]
    bins = window - MAXLAG - WINDOW_PAD
    return pl.pallas_call(
        corr_kernel,
        grid=(pairs // LANES,),
        in_specs=[
            pl.BlockSpec(own_t.shape, lambda j: (0, 0)),
            pl.BlockSpec(all_t.shape, lambda j: (0, 0)),
            pl.BlockSpec((1, LANES), lambda j: (0, j)),
            pl.BlockSpec((1, LANES), lambda j: (0, j)),
        ],
        out_specs=pl.BlockSpec((LANES, LANES), lambda j: (j, 0)),
        out_shape=jax.ShapeDtypeStruct((pairs, LANES), jnp.float32),
        scratch_shapes=[
            pltpu.VMEM((window, LANES), jnp.float32),
            pltpu.VMEM((window, LANES), jnp.float32),
            pltpu.VMEM((8, window - 8, LANES), jnp.float32),
            pltpu.VMEM((8, window - 8, LANES), jnp.float32),
            pltpu.VMEM((LANES, LANES), jnp.float32),
        ],
        cost_estimate=pl.CostEstimate(
            flops=2 * pairs * (NLAG * bins + window * (own_t.shape[1] + all_t.shape[1])),
            bytes_accessed=2 * window * (own_t.shape[1] + all_t.shape[1]) + 4 * pairs * (2 + LANES),
            transcendentals=0,
        ),
    )(own_t, all_t, first_units, second_units)


def summed_over(values, axis):
    peers = lax.axis_size(axis)
    spread = jnp.broadcast_to(values[None], (peers,) + values.shape)
    return jnp.sum(lax.all_to_all(spread, axis, 0, 0, tiled=False), axis=0)


def local(spike_sample, spike_unit, spike_amp, pair_units):
    group_index = lax.axis_index("chan")
    shard_index = lax.axis_index("tm")
    shard_count = lax.axis_size("tm")
    group_count = lax.axis_size("chan")

    bin_index = lax.div(spike_sample, SPB) - shard_index * BINS_DEV
    within = spike_unit - group_index * U_GRP
    unit_onehot = (within == lax.broadcasted_iota(jnp.int32, (U_GRP, 1), 0)).astype(jnp.bfloat16)
    weighted = jnp.where(
        bin_index == lax.broadcasted_iota(jnp.int32, (BINS_DEV, 1), 0),
        spike_amp,
        jnp.zeros((), jnp.bfloat16),
    )
    trains = lax.optimization_barrier(
        lax.dot_general(
            weighted, unit_onehot, (((1,), (1,)), ((), ())), preferred_element_type=jnp.float32
        )
    )

    unit_sums = lax.dot_general(
        unit_onehot, spike_amp, (((1,), (1,)), ((), ())), preferred_element_type=jnp.float32
    )[:, 0]

    to_next = [(i, i + 1) for i in range(shard_count - 1)]
    left_raw = lax.ppermute(trains[BINS_DEV - MAXLAG :], "tm", to_next)

    totals = summed_over(unit_sums, "tm")
    means = totals / float(BINS_DEV * shard_count)

    def centre(x):
        return (x - means[None, :]).astype(jnp.bfloat16)

    left_halo = jnp.where(shard_index > 0, centre(left_raw), jnp.zeros((), jnp.bfloat16))
    window_own = jnp.concatenate(
        [left_halo, centre(trains), jnp.zeros((WINDOW_PAD, U_GRP), jnp.bfloat16)], axis=0
    )
    border = lax.ppermute(
        window_own[:, :BORDER], "chan", [(i + 1, i) for i in range(group_count - 1)]
    )
    window = jnp.concatenate([window_own, border], axis=1)

    first_units = pair_units[0:1] - group_index * U_GRP
    second_units = pair_units[1:2] - group_index * U_GRP
    partial = lagged_products(window_own, window, first_units, second_units)

    per_shard = partial.shape[0] // shard_count
    blocks = partial.reshape(shard_count, per_shard, LANES)
    summed = jnp.sum(lax.all_to_all(blocks, "tm", 0, 0, tiled=False), axis=0)
    return summed[:, :NLAG].T


def solution(mesh):
    in_specs = (P("chan", "tm"), P("chan", "tm"), P("chan", "tm"), P(None, "chan"))
    out_specs = P(None, ("chan", "tm"))
    return jax.shard_map(local, mesh=mesh, in_specs=in_specs, out_specs=out_specs, check_vma=False)
```

```python
import jax
import jax.numpy as jnp
from jax import lax
from jax.experimental import pallas as pl
from jax.experimental.pallas import tpu as pltpu
from jax.sharding import PartitionSpec as P

U_GRP = 384
BORDER = 64
BINS_DEV = 256
MAXLAG = 50
SPB = 30
NLAG = 2 * MAXLAG + 1
LANES = 128
KCHUNK = 13
WINDOW_PAD = 6


def corr_kernel(l_ref, r_ref, o_ref, left_ref, right_ref, lags_ref):
    steps = (l_ref.shape[0] - MAXLAG) // 8
    width = left_ref.shape[1]
    for r in range(8):
        left_ref[r] = l_ref[pl.ds(r, width), :]
        right_ref[r] = r_ref[pl.ds(r, width), :]

    def lag_rows(fixed_ref, moving_ref, lags, shift_of):
        def body(i, accs):
            t = pl.multiple_of(i * 8, 8)
            fixed = fixed_ref[MAXLAG % 8, pl.ds(t + 8 * (MAXLAG // 8), 8), :]
            return tuple(
                a + fixed * moving_ref[shift_of(k) % 8, pl.ds(t + 8 * (shift_of(k) // 8), 8), :]
                for a, k in zip(accs, lags)
            )

        accs = lax.fori_loop(
            0, steps, body, tuple(jnp.zeros((8, LANES), jnp.float32) for _ in lags),
            unroll=True,
        )
        for a, k in zip(accs, lags):
            lags_ref[pl.ds(k, 1), :] = jnp.sum(a, axis=0, keepdims=True)

    for first in range(0, MAXLAG, KCHUNK):
        lag_rows(left_ref, right_ref, list(range(first, min(first + KCHUNK, MAXLAG))), lambda k: k)
    for first in range(MAXLAG, NLAG, KCHUNK):
        lag_rows(
            right_ref, left_ref, list(range(first, min(first + KCHUNK, NLAG))),
            lambda k: 2 * MAXLAG - k,
        )
    lags_ref[pl.ds(NLAG, LANES - NLAG), :] = jnp.zeros((LANES - NLAG, LANES), jnp.float32)
    o_ref[...] = lags_ref[...].T


def lagged_products(left_t, right_t):
    pairs = left_t.shape[1]
    bins = left_t.shape[0] - MAXLAG - WINDOW_PAD
    return pl.pallas_call(
        corr_kernel,
        grid=(pairs // LANES,),
        in_specs=[
            pl.BlockSpec((left_t.shape[0], LANES), lambda j: (0, j)),
            pl.BlockSpec((right_t.shape[0], LANES), lambda j: (0, j)),
        ],
        out_specs=pl.BlockSpec((LANES, LANES), lambda j: (j, 0)),
        out_shape=jax.ShapeDtypeStruct((pairs, LANES), jnp.float32),
        scratch_shapes=[
            pltpu.VMEM((8, left_t.shape[0] - 8, LANES), jnp.float32),
            pltpu.VMEM((8, left_t.shape[0] - 8, LANES), jnp.float32),
            pltpu.VMEM((LANES, LANES), jnp.float32),
        ],
        cost_estimate=pl.CostEstimate(
            flops=2 * NLAG * pairs * bins,
            bytes_accessed=4 * pairs * (left_t.shape[0] + right_t.shape[0] + LANES),
            transcendentals=0,
        ),
    )(left_t, right_t)


def summed_over(values, axis):
    peers = lax.axis_size(axis)
    spread = jnp.broadcast_to(values[None], (peers,) + values.shape)
    return jnp.sum(lax.all_to_all(spread, axis, 0, 0, tiled=False), axis=0)


def gather_columns(rows, index):
    onehot = (lax.broadcasted_iota(jnp.int32, (rows.shape[0], index.shape[0]), 0) == index[None, :])
    return lax.dot_general(
        rows, onehot.astype(rows.dtype), (((0,), (0,)), ((), ())),
        preferred_element_type=jnp.float32,
    )


def local(spike_sample, spike_unit, spike_amp, pair_units):
    group_index = lax.axis_index("chan")
    shard_index = lax.axis_index("tm")
    shard_count = lax.axis_size("tm")
    group_count = lax.axis_size("chan")

    bin_starts = SPB * (shard_index * BINS_DEV + lax.broadcasted_iota(jnp.int32, (BINS_DEV, 1), 0))
    offset = spike_sample - bin_starts
    unit_ids = group_index * U_GRP + lax.broadcasted_iota(jnp.int32, (U_GRP, 1), 0)
    unit_onehot = (spike_unit == unit_ids).astype(jnp.bfloat16)
    weighted = jnp.where(
        (offset >= 0) & (offset < SPB), spike_amp.astype(jnp.float32), 0.0
    ).astype(jnp.bfloat16)
    trains = lax.dot_general(
        unit_onehot, weighted, (((1,), (1,)), ((), ())), preferred_element_type=jnp.float32
    )

    to_next = [(i, i + 1) for i in range(shard_count - 1)]
    left_raw = lax.ppermute(trains[:, BINS_DEV - MAXLAG :], "tm", to_next)

    totals = summed_over(jnp.sum(trains, axis=1), "tm")
    means = totals / float(BINS_DEV * shard_count)

    def centre(x):
        return (x - means[:, None]).astype(jnp.bfloat16)

    left_halo = jnp.where(shard_index > 0, centre(left_raw), jnp.zeros((), jnp.bfloat16))
    window_own = jnp.concatenate(
        [left_halo, centre(trains), jnp.zeros((U_GRP, WINDOW_PAD), jnp.bfloat16)], axis=1
    )
    border = lax.ppermute(
        window_own[:BORDER], "chan", [(i + 1, i) for i in range(group_count - 1)]
    )
    window = jnp.concatenate([window_own, border], axis=0)

    first_units = pair_units[0] - group_index * U_GRP
    second_units = pair_units[1] - group_index * U_GRP
    left_t = gather_columns(window_own, first_units)
    right_t = gather_columns(window, second_units)
    partial = lagged_products(left_t, right_t)

    per_shard = partial.shape[0] // shard_count
    blocks = partial.reshape(shard_count, per_shard, LANES)
    summed = jnp.sum(lax.all_to_all(blocks, "tm", 0, 0, tiled=False), axis=0)
    return summed[:, :NLAG].T


def solution(mesh):
    in_specs = (P("chan", "tm"), P("chan", "tm"), P("chan", "tm"), P(None, "chan"))
    out_specs = P(None, ("chan", "tm"))
    return jax.shard_map(local, mesh=mesh, in_specs=in_specs, out_specs=out_specs, check_vma=False)
```

```python
import jax
import jax.numpy as jnp
from jax import lax
from jax.experimental import pallas as pl
from jax.experimental.pallas import tpu as pltpu
from jax.sharding import PartitionSpec as P

U_GRP = 384
BORDER = 64
BINS_DEV = 256
MAXLAG = 50
SPB = 30
NLAG = 2 * MAXLAG + 1
LANES = 128
KCHUNK = 13
WINDOW_PAD = 6


def corr_kernel(l_ref, r_ref, o_ref, left_ref, right_ref, lags_ref):
    steps = (l_ref.shape[0] - MAXLAG) // 8
    width = left_ref.shape[1]
    for r in range(8):
        left_ref[r] = l_ref[pl.ds(r, width), :]
        right_ref[r] = r_ref[pl.ds(r, width), :]

    def lag_rows(fixed_ref, moving_ref, lags, shift_of):
        def body(i, accs):
            t = pl.multiple_of(i * 8, 8)
            fixed = fixed_ref[MAXLAG % 8, pl.ds(t + 8 * (MAXLAG // 8), 8), :]
            return tuple(
                a + fixed * moving_ref[shift_of(k) % 8, pl.ds(t + 8 * (shift_of(k) // 8), 8), :]
                for a, k in zip(accs, lags)
            )

        accs = lax.fori_loop(
            0, steps, body, tuple(jnp.zeros((8, LANES), jnp.float32) for _ in lags),
            unroll=True,
        )
        for a, k in zip(accs, lags):
            lags_ref[pl.ds(k, 1), :] = jnp.sum(a, axis=0, keepdims=True)

    for first in range(0, MAXLAG, KCHUNK):
        lag_rows(left_ref, right_ref, list(range(first, min(first + KCHUNK, MAXLAG))), lambda k: k)
    for first in range(MAXLAG, NLAG, KCHUNK):
        lag_rows(
            right_ref, left_ref, list(range(first, min(first + KCHUNK, NLAG))),
            lambda k: 2 * MAXLAG - k,
        )
    lags_ref[pl.ds(NLAG, LANES - NLAG), :] = jnp.zeros((LANES - NLAG, LANES), jnp.float32)
    o_ref[...] = lags_ref[...].T


def lagged_products(left_t, right_t):
    pairs = left_t.shape[1]
    bins = left_t.shape[0] - MAXLAG - WINDOW_PAD
    return pl.pallas_call(
        corr_kernel,
        grid=(pairs // LANES,),
        in_specs=[
            pl.BlockSpec((left_t.shape[0], LANES), lambda j: (0, j)),
            pl.BlockSpec((right_t.shape[0], LANES), lambda j: (0, j)),
        ],
        out_specs=pl.BlockSpec((LANES, LANES), lambda j: (j, 0)),
        out_shape=jax.ShapeDtypeStruct((pairs, LANES), jnp.float32),
        scratch_shapes=[
            pltpu.VMEM((8, left_t.shape[0] - 8, LANES), jnp.float32),
            pltpu.VMEM((8, left_t.shape[0] - 8, LANES), jnp.float32),
            pltpu.VMEM((LANES, LANES), jnp.float32),
        ],
        cost_estimate=pl.CostEstimate(
            flops=2 * NLAG * pairs * bins,
            bytes_accessed=4 * pairs * (left_t.shape[0] + right_t.shape[0] + LANES),
            transcendentals=0,
        ),
    )(left_t, right_t)


def summed_over(values, axis):
    peers = lax.axis_size(axis)
    spread = jnp.broadcast_to(values[None], (peers,) + values.shape)
    return jnp.sum(lax.all_to_all(spread, axis, 0, 0, tiled=False), axis=0)


def gather_columns(rows, index):
    onehot = (lax.broadcasted_iota(jnp.int32, (rows.shape[0], index.shape[0]), 0) == index[None, :])
    return lax.dot_general(
        rows, onehot.astype(rows.dtype), (((0,), (0,)), ((), ())),
        preferred_element_type=jnp.float32,
    )


def local(spike_sample, spike_unit, spike_amp, pair_units):
    group_index = lax.axis_index("chan")
    shard_index = lax.axis_index("tm")
    shard_count = lax.axis_size("tm")
    group_count = lax.axis_size("chan")

    bin_starts = SPB * (shard_index * BINS_DEV + lax.broadcasted_iota(jnp.int32, (BINS_DEV, 1), 0))
    offset = spike_sample - bin_starts
    unit_ids = group_index * U_GRP + lax.broadcasted_iota(jnp.int32, (U_GRP, 1), 0)
    unit_onehot = (spike_unit == unit_ids).astype(jnp.bfloat16)
    weighted = jnp.where(
        (offset >= 0) & (offset < SPB), spike_amp.astype(jnp.float32), 0.0
    ).astype(jnp.bfloat16)
    trains = lax.dot_general(
        unit_onehot, weighted, (((1,), (1,)), ((), ())), preferred_element_type=jnp.float32
    )

    to_next = [(i, i + 1) for i in range(shard_count - 1)]
    left_raw = lax.ppermute(trains[:, BINS_DEV - MAXLAG :], "tm", to_next)

    totals = summed_over(jnp.sum(trains, axis=1), "tm")
    means = totals / float(BINS_DEV * shard_count)

    def centre(x):
        return (x - means[:, None]).astype(jnp.bfloat16)

    left_halo = jnp.where(shard_index > 0, centre(left_raw), jnp.zeros((), jnp.bfloat16))
    window_own = jnp.concatenate(
        [left_halo, centre(trains), jnp.zeros((U_GRP, WINDOW_PAD), jnp.bfloat16)], axis=1
    )
    border = lax.ppermute(
        window_own[:BORDER], "chan", [(i + 1, i) for i in range(group_count - 1)]
    )
    window = jnp.concatenate([window_own, border], axis=0)

    first_units = pair_units[0] - group_index * U_GRP
    second_units = pair_units[1] - group_index * U_GRP
    left_t = gather_columns(window_own, first_units)
    right_t = gather_columns(window, second_units)
    partial = lagged_products(left_t, right_t)

    per_shard = partial.shape[0] // shard_count
    blocks = partial[:, :NLAG].reshape(shard_count, 1, per_shard * NLAG)
    summed = jnp.sum(lax.all_to_all(blocks, "tm", 0, 0, tiled=False), axis=(0, 1))
    return summed.reshape(per_shard, NLAG).T


def solution(mesh):
    in_specs = (P("chan", "tm"), P("chan", "tm"), P("chan", "tm"), P(None, "chan"))
    out_specs = P(None, ("chan", "tm"))
    return jax.shard_map(local, mesh=mesh, in_specs=in_specs, out_specs=out_specs, check_vma=False)
```

```python
import jax
import jax.numpy as jnp
from jax import lax
from jax.experimental import pallas as pl
from jax.experimental.pallas import tpu as pltpu
from jax.sharding import PartitionSpec as P

U_GRP = 384
BORDER = 64
BINS_DEV = 256
MAXLAG = 50
SPB = 30
NLAG = 2 * MAXLAG + 1
LANES = 128
KCHUNK = 13
WINDOW_PAD = 14


def corr_kernel(l_ref, r_ref, o_ref, lf_ref, rf_ref, left_ref, right_ref, lags_ref):
    steps = (l_ref.shape[0] - MAXLAG - WINDOW_PAD) // 8
    width = left_ref.shape[1]
    lf_ref[...] = l_ref[...].astype(jnp.float32)
    rf_ref[...] = r_ref[...].astype(jnp.float32)
    for r in range(8):
        left_ref[r] = lf_ref[pl.ds(r, width), :]
        right_ref[r] = rf_ref[pl.ds(r, width), :]

    def lag_rows(fixed_ref, moving_ref, lags, shift_of):
        def body(i, accs):
            t = pl.multiple_of(i * 8, 8)
            fixed = fixed_ref[MAXLAG % 8, pl.ds(t + 8 * (MAXLAG // 8), 8), :]
            return tuple(
                a + fixed * moving_ref[shift_of(k) % 8, pl.ds(t + 8 * (shift_of(k) // 8), 8), :]
                for a, k in zip(accs, lags)
            )

        accs = lax.fori_loop(
            0, steps, body, tuple(jnp.zeros((8, LANES), jnp.float32) for _ in lags),
            unroll=True,
        )
        for a, k in zip(accs, lags):
            lags_ref[pl.ds(k, 1), :] = jnp.sum(a, axis=0, keepdims=True)

    for first in range(0, MAXLAG, KCHUNK):
        lag_rows(left_ref, right_ref, list(range(first, min(first + KCHUNK, MAXLAG))), lambda k: k)
    for first in range(MAXLAG, NLAG, KCHUNK):
        lag_rows(
            right_ref, left_ref, list(range(first, min(first + KCHUNK, NLAG))),
            lambda k: 2 * MAXLAG - k,
        )
    lags_ref[pl.ds(NLAG, LANES - NLAG), :] = jnp.zeros((LANES - NLAG, LANES), jnp.float32)
    o_ref[...] = lags_ref[...].T


def lagged_products(left_t, right_t):
    pairs = left_t.shape[1]
    bins = left_t.shape[0] - MAXLAG - WINDOW_PAD
    return pl.pallas_call(
        corr_kernel,
        grid=(pairs // LANES,),
        in_specs=[
            pl.BlockSpec((left_t.shape[0], LANES), lambda j: (0, j)),
            pl.BlockSpec((right_t.shape[0], LANES), lambda j: (0, j)),
        ],
        out_specs=pl.BlockSpec((LANES, LANES), lambda j: (j, 0)),
        out_shape=jax.ShapeDtypeStruct((pairs, LANES), jnp.float32),
        scratch_shapes=[
            pltpu.VMEM((left_t.shape[0], LANES), jnp.float32),
            pltpu.VMEM((left_t.shape[0], LANES), jnp.float32),
            pltpu.VMEM((8, left_t.shape[0] - 8, LANES), jnp.float32),
            pltpu.VMEM((8, left_t.shape[0] - 8, LANES), jnp.float32),
            pltpu.VMEM((LANES, LANES), jnp.float32),
        ],
        cost_estimate=pl.CostEstimate(
            flops=2 * NLAG * pairs * bins,
            bytes_accessed=pairs * (2 * left_t.shape[0] + 2 * right_t.shape[0] + 4 * LANES),
            transcendentals=0,
        ),
    )(left_t, right_t)


def summed_over(values, axis):
    peers = lax.axis_size(axis)
    spread = jnp.broadcast_to(values[None], (peers,) + values.shape)
    return jnp.sum(lax.all_to_all(spread, axis, 0, 0, tiled=False), axis=0)


def gather_columns(rows, index):
    onehot = (lax.broadcasted_iota(jnp.int32, (rows.shape[0], index.shape[0]), 0) == index[None, :])
    return lax.dot_general(
        rows, onehot.astype(rows.dtype), (((0,), (0,)), ((), ())),
        preferred_element_type=jnp.float32,
    ).astype(rows.dtype)


def local(spike_sample, spike_unit, spike_amp, pair_units):
    group_index = lax.axis_index("chan")
    shard_index = lax.axis_index("tm")
    shard_count = lax.axis_size("tm")
    group_count = lax.axis_size("chan")

    bin_starts = SPB * (shard_index * BINS_DEV + lax.broadcasted_iota(jnp.int32, (BINS_DEV, 1), 0))
    offset = spike_sample - bin_starts
    unit_ids = group_index * U_GRP + lax.broadcasted_iota(jnp.int32, (U_GRP, 1), 0)
    unit_onehot = (spike_unit == unit_ids).astype(jnp.bfloat16)
    weighted = jnp.where(
        (offset >= 0) & (offset < SPB), spike_amp.astype(jnp.float32), 0.0
    ).astype(jnp.bfloat16)
    trains = lax.dot_general(
        unit_onehot, weighted, (((1,), (1,)), ((), ())), preferred_element_type=jnp.float32
    )

    to_next = [(i, i + 1) for i in range(shard_count - 1)]
    left_raw = lax.ppermute(trains[:, BINS_DEV - MAXLAG :], "tm", to_next)

    totals = summed_over(jnp.sum(trains, axis=1), "tm")
    means = totals / float(BINS_DEV * shard_count)

    def centre(x):
        return (x - means[:, None]).astype(jnp.bfloat16)

    left_halo = jnp.where(shard_index > 0, centre(left_raw), jnp.zeros((), jnp.bfloat16))
    window_own = jnp.concatenate(
        [left_halo, centre(trains), jnp.zeros((U_GRP, WINDOW_PAD), jnp.bfloat16)], axis=1
    )
    border = lax.ppermute(
        window_own[:BORDER], "chan", [(i + 1, i) for i in range(group_count - 1)]
    )
    window = jnp.concatenate([window_own, border], axis=0)

    first_units = pair_units[0] - group_index * U_GRP
    second_units = pair_units[1] - group_index * U_GRP
    left_t = gather_columns(window_own, first_units)
    right_t = gather_columns(window, second_units)
    partial = lagged_products(left_t, right_t)

    per_shard = partial.shape[0] // shard_count
    blocks = partial.reshape(shard_count, per_shard, LANES)
    summed = jnp.sum(lax.all_to_all(blocks, "tm", 0, 0, tiled=False), axis=0)
    return summed[:, :NLAG].T


def solution(mesh):
    in_specs = (P("chan", "tm"), P("chan", "tm"), P("chan", "tm"), P(None, "chan"))
    out_specs = P(None, ("chan", "tm"))
    return jax.shard_map(local, mesh=mesh, in_specs=in_specs, out_specs=out_specs, check_vma=False)
```

```python
import jax
import jax.numpy as jnp
from jax import lax
from jax.experimental import pallas as pl
from jax.experimental.pallas import tpu as pltpu
from jax.sharding import PartitionSpec as P

U_GRP = 384
BORDER = 64
BINS_DEV = 256
MAXLAG = 50
SPB = 30
NLAG = 2 * MAXLAG + 1
LANES = 128
KCHUNK = 13
WINDOW_PAD = 14


def corr_kernel(l_ref, r_ref, o_ref, lf_ref, rf_ref, left_ref, right_ref, lags_ref):
    steps = (l_ref.shape[0] - MAXLAG - WINDOW_PAD) // 8
    width = left_ref.shape[1]
    lf_ref[...] = l_ref[...].astype(jnp.float32)
    rf_ref[...] = r_ref[...].astype(jnp.float32)
    for r in range(8):
        left_ref[r] = lf_ref[pl.ds(r, width), :]
        right_ref[r] = rf_ref[pl.ds(r, width), :]

    def lag_rows(fixed_ref, moving_ref, lags, shift_of):
        def body(i, accs):
            t = pl.multiple_of(i * 8, 8)
            fixed = fixed_ref[MAXLAG % 8, pl.ds(t + 8 * (MAXLAG // 8), 8), :]
            return tuple(
                a + fixed * moving_ref[shift_of(k) % 8, pl.ds(t + 8 * (shift_of(k) // 8), 8), :]
                for a, k in zip(accs, lags)
            )

        accs = lax.fori_loop(
            0, steps, body, tuple(jnp.zeros((8, LANES), jnp.float32) for _ in lags),
            unroll=True,
        )
        for a, k in zip(accs, lags):
            lags_ref[pl.ds(k, 1), :] = jnp.sum(a, axis=0, keepdims=True)

    for first in range(0, MAXLAG, KCHUNK):
        lag_rows(left_ref, right_ref, list(range(first, min(first + KCHUNK, MAXLAG))), lambda k: k)
    for first in range(MAXLAG, NLAG, KCHUNK):
        lag_rows(
            right_ref, left_ref, list(range(first, min(first + KCHUNK, NLAG))),
            lambda k: 2 * MAXLAG - k,
        )
    lags_ref[pl.ds(NLAG, LANES - NLAG), :] = jnp.zeros((LANES - NLAG, LANES), jnp.float32)
    o_ref[...] = lags_ref[...].T


def lagged_products(left_t, right_t):
    pairs = left_t.shape[1]
    bins = left_t.shape[0] - MAXLAG - WINDOW_PAD
    return pl.pallas_call(
        corr_kernel,
        grid=(pairs // LANES,),
        in_specs=[
            pl.BlockSpec((left_t.shape[0], LANES), lambda j: (0, j)),
            pl.BlockSpec((right_t.shape[0], LANES), lambda j: (0, j)),
        ],
        out_specs=pl.BlockSpec((LANES, LANES), lambda j: (j, 0)),
        out_shape=jax.ShapeDtypeStruct((pairs, LANES), jnp.float32),
        scratch_shapes=[
            pltpu.VMEM((left_t.shape[0], LANES), jnp.float32),
            pltpu.VMEM((left_t.shape[0], LANES), jnp.float32),
            pltpu.VMEM((8, left_t.shape[0] - 8, LANES), jnp.float32),
            pltpu.VMEM((8, left_t.shape[0] - 8, LANES), jnp.float32),
            pltpu.VMEM((LANES, LANES), jnp.float32),
        ],
        cost_estimate=pl.CostEstimate(
            flops=2 * NLAG * pairs * bins,
            bytes_accessed=pairs * (2 * left_t.shape[0] + 2 * right_t.shape[0] + 4 * LANES),
            transcendentals=0,
        ),
    )(left_t, right_t)


def summed_over(values, axis):
    peers = lax.axis_size(axis)
    spread = jnp.broadcast_to(values[None], (peers,) + values.shape)
    return jnp.sum(lax.all_to_all(spread, axis, 0, 0, tiled=False), axis=0)


def gather_columns(rows, index):
    onehot = (lax.broadcasted_iota(jnp.int32, (rows.shape[0], index.shape[0]), 0) == index[None, :])
    return lax.dot_general(
        rows, onehot.astype(rows.dtype), (((0,), (0,)), ((), ())),
        preferred_element_type=jnp.float32,
    ).astype(rows.dtype)


def local(spike_sample, spike_unit, spike_amp, pair_units):
    group_index = lax.axis_index("chan")
    shard_index = lax.axis_index("tm")
    shard_count = lax.axis_size("tm")
    group_count = lax.axis_size("chan")

    bin_starts = SPB * (shard_index * BINS_DEV + lax.broadcasted_iota(jnp.int32, (BINS_DEV, 1), 0))
    offset = spike_sample - bin_starts
    unit_ids = group_index * U_GRP + lax.broadcasted_iota(jnp.int32, (U_GRP, 1), 0)
    unit_onehot = (spike_unit == unit_ids).astype(jnp.bfloat16)
    weighted = jnp.where(
        (offset >= 0) & (offset < SPB), spike_amp.astype(jnp.float32), 0.0
    ).astype(jnp.bfloat16)
    trains = lax.dot_general(
        unit_onehot, weighted, (((1,), (1,)), ((), ())), preferred_element_type=jnp.float32
    )

    to_next = [(i, i + 1) for i in range(shard_count - 1)]
    left_raw = lax.ppermute(trains[:, BINS_DEV - MAXLAG :], "tm", to_next)

    totals = summed_over(jnp.sum(trains, axis=1), "tm")
    means = totals / float(BINS_DEV * shard_count)

    def centre(x):
        return (x - means[:, None]).astype(jnp.bfloat16)

    left_halo = jnp.where(shard_index > 0, centre(left_raw), jnp.zeros((), jnp.bfloat16))
    window_own = jnp.concatenate(
        [left_halo, centre(trains), jnp.zeros((U_GRP, WINDOW_PAD), jnp.bfloat16)], axis=1
    )
    first_units = pair_units[0] - group_index * U_GRP
    second_units = pair_units[1] - group_index * U_GRP
    left_t, sent = lax.optimization_barrier(
        (gather_columns(window_own, first_units), window_own[:BORDER])
    )
    border = lax.ppermute(sent, "chan", [(i + 1, i) for i in range(group_count - 1)])
    window = jnp.concatenate([window_own, border], axis=0)
    right_t = gather_columns(window, second_units)
    partial = lagged_products(left_t, right_t)

    per_shard = partial.shape[0] // shard_count
    blocks = partial.reshape(shard_count, per_shard, LANES)
    summed = jnp.sum(lax.all_to_all(blocks, "tm", 0, 0, tiled=False), axis=0)
    return summed[:, :NLAG].T


def solution(mesh):
    in_specs = (P("chan", "tm"), P("chan", "tm"), P("chan", "tm"), P(None, "chan"))
    out_specs = P(None, ("chan", "tm"))
    return jax.shard_map(local, mesh=mesh, in_specs=in_specs, out_specs=out_specs, check_vma=False)
```

```python
import jax
import jax.numpy as jnp
from jax import lax
from jax.experimental import pallas as pl
from jax.experimental.pallas import tpu as pltpu
from jax.sharding import PartitionSpec as P

U_GRP = 384
BORDER = 64
BINS_DEV = 256
MAXLAG = 50
SPB = 30
NLAG = 2 * MAXLAG + 1
LANES = 128
KCHUNK = 13
WINDOW_PAD = 14
STEP_BLOCKS = 2


def corr_kernel(l_ref, r_ref, o_ref, lf_ref, rf_ref, left_ref, right_ref, lags_ref):
    for sub in range(l_ref.shape[1] // LANES):
        lane_block(l_ref, r_ref, o_ref, lf_ref, rf_ref, left_ref, right_ref, lags_ref, sub)


def lane_block(l_ref, r_ref, o_ref, lf_ref, rf_ref, left_ref, right_ref, lags_ref, sub):
    lanes = pl.ds(sub * LANES, LANES)
    steps = (l_ref.shape[0] - MAXLAG - WINDOW_PAD) // 8
    width = left_ref.shape[1]
    lf_ref[...] = l_ref[:, lanes].astype(jnp.float32)
    rf_ref[...] = r_ref[:, lanes].astype(jnp.float32)
    for r in range(8):
        left_ref[r] = lf_ref[pl.ds(r, width), :]
        right_ref[r] = rf_ref[pl.ds(r, width), :]

    def lag_rows(fixed_ref, moving_ref, lags, shift_of):
        def body(i, accs):
            t = pl.multiple_of(i * 8, 8)
            fixed = fixed_ref[MAXLAG % 8, pl.ds(t + 8 * (MAXLAG // 8), 8), :]
            return tuple(
                a + fixed * moving_ref[shift_of(k) % 8, pl.ds(t + 8 * (shift_of(k) // 8), 8), :]
                for a, k in zip(accs, lags)
            )

        accs = lax.fori_loop(
            0, steps, body, tuple(jnp.zeros((8, LANES), jnp.float32) for _ in lags),
            unroll=True,
        )
        for a, k in zip(accs, lags):
            lags_ref[pl.ds(k, 1), :] = jnp.sum(a, axis=0, keepdims=True)

    for first in range(0, MAXLAG, KCHUNK):
        lag_rows(left_ref, right_ref, list(range(first, min(first + KCHUNK, MAXLAG))), lambda k: k)
    for first in range(MAXLAG, NLAG, KCHUNK):
        lag_rows(
            right_ref, left_ref, list(range(first, min(first + KCHUNK, NLAG))),
            lambda k: 2 * MAXLAG - k,
        )
    lags_ref[pl.ds(NLAG, LANES - NLAG), :] = jnp.zeros((LANES - NLAG, LANES), jnp.float32)
    o_ref[pl.ds(sub * LANES, LANES), :] = lags_ref[...].T


def lagged_products(left_t, right_t):
    pairs = left_t.shape[1]
    bins = left_t.shape[0] - MAXLAG - WINDOW_PAD
    return pl.pallas_call(
        corr_kernel,
        grid=(pairs // (LANES * STEP_BLOCKS),),
        in_specs=[
            pl.BlockSpec((left_t.shape[0], LANES * STEP_BLOCKS), lambda j: (0, j)),
            pl.BlockSpec((right_t.shape[0], LANES * STEP_BLOCKS), lambda j: (0, j)),
        ],
        out_specs=pl.BlockSpec((LANES * STEP_BLOCKS, LANES), lambda j: (j, 0)),
        out_shape=jax.ShapeDtypeStruct((pairs, LANES), jnp.float32),
        scratch_shapes=[
            pltpu.VMEM((left_t.shape[0], LANES), jnp.float32),
            pltpu.VMEM((left_t.shape[0], LANES), jnp.float32),
            pltpu.VMEM((8, left_t.shape[0] - 8, LANES), jnp.float32),
            pltpu.VMEM((8, left_t.shape[0] - 8, LANES), jnp.float32),
            pltpu.VMEM((LANES, LANES), jnp.float32),
        ],
        cost_estimate=pl.CostEstimate(
            flops=2 * NLAG * pairs * bins,
            bytes_accessed=pairs * (2 * left_t.shape[0] + 2 * right_t.shape[0] + 4 * LANES),
            transcendentals=0,
        ),
    )(left_t, right_t)


def summed_over(values, axis):
    peers = lax.axis_size(axis)
    spread = jnp.broadcast_to(values[None], (peers,) + values.shape)
    return jnp.sum(lax.all_to_all(spread, axis, 0, 0, tiled=False), axis=0)


def gather_columns(rows, index):
    onehot = (lax.broadcasted_iota(jnp.int32, (rows.shape[0], index.shape[0]), 0) == index[None, :])
    return lax.dot_general(
        rows, onehot.astype(rows.dtype), (((0,), (0,)), ((), ())),
        preferred_element_type=jnp.float32,
    ).astype(rows.dtype)


def local(spike_sample, spike_unit, spike_amp, pair_units):
    group_index = lax.axis_index("chan")
    shard_index = lax.axis_index("tm")
    shard_count = lax.axis_size("tm")
    group_count = lax.axis_size("chan")

    bin_starts = SPB * (shard_index * BINS_DEV + lax.broadcasted_iota(jnp.int32, (BINS_DEV, 1), 0))
    offset = spike_sample - bin_starts
    unit_ids = group_index * U_GRP + lax.broadcasted_iota(jnp.int32, (U_GRP, 1), 0)
    unit_onehot = (spike_unit == unit_ids).astype(jnp.bfloat16)
    weighted = jnp.where(
        (offset >= 0) & (offset < SPB), spike_amp.astype(jnp.float32), 0.0
    ).astype(jnp.bfloat16)
    trains = lax.dot_general(
        unit_onehot, weighted, (((1,), (1,)), ((), ())), preferred_element_type=jnp.float32
    )

    to_next = [(i, i + 1) for i in range(shard_count - 1)]
    left_raw = lax.ppermute(trains[:, BINS_DEV - MAXLAG :], "tm", to_next)

    totals = summed_over(jnp.sum(trains, axis=1), "tm")
    means = totals / float(BINS_DEV * shard_count)

    def centre(x):
        return (x - means[:, None]).astype(jnp.bfloat16)

    left_halo = jnp.where(shard_index > 0, centre(left_raw), jnp.zeros((), jnp.bfloat16))
    window_own = jnp.concatenate(
        [left_halo, centre(trains), jnp.zeros((U_GRP, WINDOW_PAD), jnp.bfloat16)], axis=1
    )
    border = lax.ppermute(
        window_own[:BORDER], "chan", [(i + 1, i) for i in range(group_count - 1)]
    )
    window = jnp.concatenate([window_own, border], axis=0)

    first_units = pair_units[0] - group_index * U_GRP
    second_units = pair_units[1] - group_index * U_GRP
    left_t = gather_columns(window_own, first_units)
    right_t = gather_columns(window, second_units)
    partial = lagged_products(left_t, right_t)

    per_shard = partial.shape[0] // shard_count
    blocks = partial.reshape(shard_count, per_shard, LANES)
    summed = jnp.sum(lax.all_to_all(blocks, "tm", 0, 0, tiled=False), axis=0)
    return summed[:, :NLAG].T


def solution(mesh):
    in_specs = (P("chan", "tm"), P("chan", "tm"), P("chan", "tm"), P(None, "chan"))
    out_specs = P(None, ("chan", "tm"))
    return jax.shard_map(local, mesh=mesh, in_specs=in_specs, out_specs=out_specs, check_vma=False)
```

```python
import jax
import jax.numpy as jnp
from jax import lax
from jax.experimental import pallas as pl
from jax.experimental.pallas import tpu as pltpu
from jax.sharding import PartitionSpec as P

U_GRP = 384
BORDER = 64
BINS_DEV = 256
MAXLAG = 50
SPB = 30
NLAG = 2 * MAXLAG + 1
LANES = 128
KCHUNK = 13
WINDOW_PAD = 14


def corr_kernel(l_ref, r_ref, o_ref, lf_ref, rf_ref, left_ref, right_ref, lags_ref):
    steps = (l_ref.shape[0] - MAXLAG - WINDOW_PAD) // 8
    width = left_ref.shape[1]
    lf_ref[...] = l_ref[...].astype(jnp.float32)
    rf_ref[...] = r_ref[...].astype(jnp.float32)
    for r in range(1, 8):
        left_ref[r] = lf_ref[pl.ds(r, width), :]
        right_ref[r] = rf_ref[pl.ds(r, width), :]

    def lag_rows(fixed_ref, moving_ref, moving_flat, lags, shift_of):
        def moved(shift, t):
            rows = pl.ds(t + 8 * (shift // 8), 8)
            return moving_flat[rows, :] if shift % 8 == 0 else moving_ref[shift % 8, rows, :]

        def body(i, accs):
            t = pl.multiple_of(i * 8, 8)
            fixed = fixed_ref[MAXLAG % 8, pl.ds(t + 8 * (MAXLAG // 8), 8), :]
            return tuple(a + fixed * moved(shift_of(k), t) for a, k in zip(accs, lags))

        accs = lax.fori_loop(
            0, steps, body, tuple(jnp.zeros((8, LANES), jnp.float32) for _ in lags),
            unroll=True,
        )
        for a, k in zip(accs, lags):
            lags_ref[pl.ds(k, 1), :] = jnp.sum(a, axis=0, keepdims=True)

    for first in range(0, MAXLAG, KCHUNK):
        lag_rows(
            left_ref, right_ref, rf_ref, list(range(first, min(first + KCHUNK, MAXLAG))),
            lambda k: k,
        )
    for first in range(MAXLAG, NLAG, KCHUNK):
        lag_rows(
            right_ref, left_ref, lf_ref, list(range(first, min(first + KCHUNK, NLAG))),
            lambda k: 2 * MAXLAG - k,
        )
    lags_ref[pl.ds(NLAG, LANES - NLAG), :] = jnp.zeros((LANES - NLAG, LANES), jnp.float32)
    o_ref[...] = lags_ref[...].T


def lagged_products(left_t, right_t):
    pairs = left_t.shape[1]
    bins = left_t.shape[0] - MAXLAG - WINDOW_PAD
    return pl.pallas_call(
        corr_kernel,
        grid=(pairs // LANES,),
        in_specs=[
            pl.BlockSpec((left_t.shape[0], LANES), lambda j: (0, j)),
            pl.BlockSpec((right_t.shape[0], LANES), lambda j: (0, j)),
        ],
        out_specs=pl.BlockSpec((LANES, LANES), lambda j: (j, 0)),
        out_shape=jax.ShapeDtypeStruct((pairs, LANES), jnp.float32),
        scratch_shapes=[
            pltpu.VMEM((left_t.shape[0], LANES), jnp.float32),
            pltpu.VMEM((left_t.shape[0], LANES), jnp.float32),
            pltpu.VMEM((8, left_t.shape[0] - 8, LANES), jnp.float32),
            pltpu.VMEM((8, left_t.shape[0] - 8, LANES), jnp.float32),
            pltpu.VMEM((LANES, LANES), jnp.float32),
        ],
        cost_estimate=pl.CostEstimate(
            flops=2 * NLAG * pairs * bins,
            bytes_accessed=pairs * (2 * left_t.shape[0] + 2 * right_t.shape[0] + 4 * LANES),
            transcendentals=0,
        ),
    )(left_t, right_t)


def summed_over(values, axis):
    peers = lax.axis_size(axis)
    spread = jnp.broadcast_to(values[None], (peers,) + values.shape)
    return jnp.sum(lax.all_to_all(spread, axis, 0, 0, tiled=False), axis=0)


def gather_columns(rows, index):
    onehot = (lax.broadcasted_iota(jnp.int32, (rows.shape[0], index.shape[0]), 0) == index[None, :])
    return lax.dot_general(
        rows, onehot.astype(rows.dtype), (((0,), (0,)), ((), ())),
        preferred_element_type=jnp.float32,
    ).astype(rows.dtype)


def local(spike_sample, spike_unit, spike_amp, pair_units):
    group_index = lax.axis_index("chan")
    shard_index = lax.axis_index("tm")
    shard_count = lax.axis_size("tm")
    group_count = lax.axis_size("chan")

    bin_starts = SPB * (shard_index * BINS_DEV + lax.broadcasted_iota(jnp.int32, (BINS_DEV, 1), 0))
    offset = spike_sample - bin_starts
    unit_ids = group_index * U_GRP + lax.broadcasted_iota(jnp.int32, (U_GRP, 1), 0)
    unit_onehot = (spike_unit == unit_ids).astype(jnp.bfloat16)
    weighted = jnp.where(
        (offset >= 0) & (offset < SPB), spike_amp.astype(jnp.float32), 0.0
    ).astype(jnp.bfloat16)
    trains = lax.dot_general(
        unit_onehot, weighted, (((1,), (1,)), ((), ())), preferred_element_type=jnp.float32
    )

    to_next = [(i, i + 1) for i in range(shard_count - 1)]
    left_raw = lax.ppermute(trains[:, BINS_DEV - MAXLAG :], "tm", to_next)

    totals = summed_over(jnp.sum(trains, axis=1), "tm")
    means = totals / float(BINS_DEV * shard_count)

    def centre(x):
        return (x - means[:, None]).astype(jnp.bfloat16)

    left_halo = jnp.where(shard_index > 0, centre(left_raw), jnp.zeros((), jnp.bfloat16))
    window_own = jnp.concatenate(
        [left_halo, centre(trains), jnp.zeros((U_GRP, WINDOW_PAD), jnp.bfloat16)], axis=1
    )
    border = lax.ppermute(
        window_own[:BORDER], "chan", [(i + 1, i) for i in range(group_count - 1)]
    )
    window = jnp.concatenate([window_own, border], axis=0)

    first_units = pair_units[0] - group_index * U_GRP
    second_units = pair_units[1] - group_index * U_GRP
    left_t = gather_columns(window_own, first_units)
    right_t = gather_columns(window, second_units)
    partial = lagged_products(left_t, right_t)

    per_shard = partial.shape[0] // shard_count
    blocks = partial.reshape(shard_count, per_shard, LANES)
    summed = jnp.sum(lax.all_to_all(blocks, "tm", 0, 0, tiled=False), axis=0)
    return summed[:, :NLAG].T


def solution(mesh):
    in_specs = (P("chan", "tm"), P("chan", "tm"), P("chan", "tm"), P(None, "chan"))
    out_specs = P(None, ("chan", "tm"))
    return jax.shard_map(local, mesh=mesh, in_specs=in_specs, out_specs=out_specs, check_vma=False)
```

```python
import jax
import jax.numpy as jnp
from jax import lax
from jax.experimental import pallas as pl
from jax.experimental.pallas import tpu as pltpu
from jax.sharding import PartitionSpec as P

U_GRP = 384
BORDER = 64
BINS_DEV = 256
MAXLAG = 50
SPB = 30
NLAG = 2 * MAXLAG + 1
LANES = 128
KCHUNK = 13
WINDOW_PAD = 14


def corr_kernel(l_ref, r_ref, o_ref, lf_ref, rf_ref, left_ref, right_ref, lags_ref):
    steps = (l_ref.shape[0] - MAXLAG - WINDOW_PAD) // 8
    width = left_ref.shape[1]
    lf_ref[...] = l_ref[...].astype(jnp.float32)
    rf_ref[...] = r_ref[...].astype(jnp.float32)
    for r in range(8):
        left_ref[r] = lf_ref[pl.ds(r, width), :]
        right_ref[r] = rf_ref[pl.ds(r, width), :]

    def lag_rows(fixed_ref, moving_ref, lags, shift_of):
        def body(i, accs):
            t = pl.multiple_of(i * 8, 8)
            fixed = fixed_ref[MAXLAG % 8, pl.ds(t + 8 * (MAXLAG // 8), 8), :]
            return tuple(
                a + fixed * moving_ref[shift_of(k) % 8, pl.ds(t + 8 * (shift_of(k) // 8), 8), :]
                for a, k in zip(accs, lags)
            )

        accs = lax.fori_loop(
            0, steps, body, tuple(jnp.zeros((8, LANES), jnp.float32) for _ in lags),
            unroll=True,
        )
        for a, k in zip(accs, lags):
            lags_ref[pl.ds(k, 1), :] = jnp.sum(a, axis=0, keepdims=True)

    for first in range(0, MAXLAG, KCHUNK):
        lag_rows(left_ref, right_ref, list(range(first, min(first + KCHUNK, MAXLAG))), lambda k: k)
    for first in range(MAXLAG, NLAG, KCHUNK):
        lag_rows(
            right_ref, left_ref, list(range(first, min(first + KCHUNK, NLAG))),
            lambda k: 2 * MAXLAG - k,
        )
    lags_ref[pl.ds(NLAG, LANES - NLAG), :] = jnp.zeros((LANES - NLAG, LANES), jnp.float32)
    o_ref[...] = lags_ref[...].T


def lagged_products(left_t, right_t):
    pairs = left_t.shape[1]
    bins = left_t.shape[0] - MAXLAG - WINDOW_PAD
    return pl.pallas_call(
        corr_kernel,
        grid=(pairs // LANES,),
        in_specs=[
            pl.BlockSpec((left_t.shape[0], LANES), lambda j: (0, j)),
            pl.BlockSpec((right_t.shape[0], LANES), lambda j: (0, j)),
        ],
        out_specs=pl.BlockSpec((LANES, LANES), lambda j: (j, 0)),
        out_shape=jax.ShapeDtypeStruct((pairs, LANES), jnp.float32),
        scratch_shapes=[
            pltpu.VMEM((left_t.shape[0], LANES), jnp.float32),
            pltpu.VMEM((left_t.shape[0], LANES), jnp.float32),
            pltpu.VMEM((8, left_t.shape[0] - 8, LANES), jnp.float32),
            pltpu.VMEM((8, left_t.shape[0] - 8, LANES), jnp.float32),
            pltpu.VMEM((LANES, LANES), jnp.float32),
        ],
        cost_estimate=pl.CostEstimate(
            flops=2 * NLAG * pairs * bins,
            bytes_accessed=pairs * (2 * left_t.shape[0] + 2 * right_t.shape[0] + 4 * LANES),
            transcendentals=0,
        ),
    )(left_t, right_t)


def summed_over(values, axis):
    peers = lax.axis_size(axis)
    spread = jnp.broadcast_to(values[None], (peers,) + values.shape)
    return jnp.sum(lax.all_to_all(spread, axis, 0, 0, tiled=False), axis=0)


def gather_columns(rows, index):
    onehot = (lax.broadcasted_iota(jnp.int32, (rows.shape[0], index.shape[0]), 0) == index[None, :])
    return lax.dot_general(
        rows, onehot.astype(rows.dtype), (((0,), (0,)), ((), ())),
        preferred_element_type=jnp.float32,
    ).astype(rows.dtype)


def local(spike_sample, spike_unit, spike_amp, pair_units):
    group_index = lax.axis_index("chan")
    shard_index = lax.axis_index("tm")
    shard_count = lax.axis_size("tm")
    group_count = lax.axis_size("chan")

    bin_starts = SPB * (shard_index * BINS_DEV + lax.broadcasted_iota(jnp.int32, (BINS_DEV, 1), 0))
    offset = spike_sample - bin_starts
    unit_ids = group_index * U_GRP + lax.broadcasted_iota(jnp.int32, (U_GRP, 1), 0)
    unit_onehot = (spike_unit == unit_ids).astype(jnp.bfloat16)
    weighted = jnp.where(
        (offset >= 0) & (offset < SPB), spike_amp.astype(jnp.float32), 0.0
    ).astype(jnp.bfloat16)
    trains = lax.dot_general(
        unit_onehot, weighted, (((1,), (1,)), ((), ())), preferred_element_type=jnp.float32
    )

    to_next = [(i, i + 1) for i in range(shard_count - 1)]
    left_raw = lax.ppermute(trains[:, BINS_DEV - MAXLAG :], "tm", to_next)

    totals = summed_over(jnp.sum(trains, axis=1), "tm")
    means = totals / float(BINS_DEV * shard_count)

    def centre(x):
        return (x - means[:, None]).astype(jnp.bfloat16)

    left_halo = jnp.where(shard_index > 0, centre(left_raw), jnp.zeros((), jnp.bfloat16))
    window_own = jnp.concatenate(
        [left_halo, centre(trains), jnp.zeros((U_GRP, WINDOW_PAD), jnp.bfloat16)], axis=1
    )
    border = lax.ppermute(
        window_own[:BORDER], "chan", [(i + 1, i) for i in range(group_count - 1)]
    )
    window = jnp.concatenate([window_own, border], axis=0)

    first_units = pair_units[0] - group_index * U_GRP
    second_units = pair_units[1] - group_index * U_GRP
    left_t = gather_columns(window_own, first_units)
    right_t = gather_columns(window, second_units)
    partial = lagged_products(left_t, right_t)

    per_shard = partial.shape[0] // shard_count
    blocks = partial.reshape(shard_count, 1, per_shard * LANES)
    summed = jnp.sum(lax.all_to_all(blocks, "tm", 0, 0, tiled=False), axis=(0, 1))
    return summed.reshape(per_shard, LANES)[:, :NLAG].T


def solution(mesh):
    in_specs = (P("chan", "tm"), P("chan", "tm"), P("chan", "tm"), P(None, "chan"))
    out_specs = P(None, ("chan", "tm"))
    return jax.shard_map(local, mesh=mesh, in_specs=in_specs, out_specs=out_specs, check_vma=False)
```
